128 devices in a mesh: grp: 2 (over core), fsdp: 64 (over x, y, z).
Axes of the slice: x: 4, y: 4, z: 4, core: 2. Of those that a mesh axis runs over, the one named last changes fastest.
Arguments:
- item_states: bfloat16 [512, 256, 2048], P(('grp', 'fsdp')), may hold values from -6 to 6
- w_query: bfloat16 [2048, 2048], P('fsdp'), may hold values from -0.125 to 0.125
- w_key: bfloat16 [2048, 256], P('fsdp'), may hold values from -0.125 to 0.125
- w_value: bfloat16 [2048, 256], P('fsdp'), may hold values from -0.125 to 0.125
- item_gain: float32 [2048], replicated, may hold values from 0.25 to 1.75
- w_adapt: bfloat16 [2048, 4096], P('fsdp'), may hold values from -0.125 to 0.125
- user_gain: float32 [4096], replicated, may hold values from 0.25 to 1.75
- user_query: bfloat16 [4096, 128], P('fsdp'), may hold values from -0.5 to 0.5
- hist_owner: int32 [128, 128, 1], P(('grp', 'fsdp')), may hold values from 0 to 127; in each aligned block of 128 rows (0 to 127, 128 to 255, ..., all dimensions but the last counted through in order) at most 2 rows name the same one
- history_position_index: int32 [128, 128], P(('grp', 'fsdp')), may hold values from 0 to 3
- cotangent: bfloat16 [128, 128, 4096], P(('grp', 'fsdp')), may hold values from -6 to 6
Outputs:
- item_embed: bfloat16 [512, 2048], P(('grp', 'fsdp'))
- user_attention_output: bfloat16 [128, 128, 4096], P(('grp', 'fsdp'))
- item_grad: float32 [512, 2048], P(('grp', 'fsdp'))
The draws below stay inside these ranges and needn't reach their ends.
Inputs may be any that keep to these rules, and one draw needn't show every extreme that they name: `hist_owner`: within one history no device is named by more than 2 positions, and some device is named by exactly 2 positions.
All inputs are finite; a program needn't handle non-finite values.
Results may differ from the reference program's by a relative error of at most 0.011.
Values may be sent and summed in bfloat16 or wider, within the bound.
No kernel may reach another device: no remote copies, remote signals or barrier semaphores. Data moves between devices by JAX's collectives and lax.ppermute only.
A program may use at most 128 MiB of HBM per device.

```python
import math
import jax
import jax.numpy as jnp
import numpy as np
from jax import lax

DI = 2048
IHEADS = 32
IHD = 64
IKV = 4
DU = 4096
UHEADS = 32
UHD = 128
ILEN = 256
ITEMS_DEV = 4
LEN = 128
ITEMS = 512
SEQS = 128
CAP = 2
N_GRP = 2
N_FSDP = 64
DEVICES = 128


def with_ends(array, rng, smallest, top_value):
    longest = array.shape.index(max(array.shape))
    spots = []
    for shift in (0, 1):
        where = [jax.random.randint(jax.random.fold_in(rng, axis), (), 0, length) for axis, length in enumerate(array.shape)]
        where[longest] = (where[longest] + shift) % array.shape[longest]
        spots.append(tuple(where))
    return array.at[spots[0]].set(smallest).at[spots[1]].set(top_value)


def block_scale(stream_key, shape, pieces, smallest, largest):
    loudness, own = 1.0, jax.random.fold_in(stream_key, 6)
    for dim, shards_of in pieces:
        draws = jnp.exp(jax.random.uniform(jax.random.fold_in(own, dim), (shards_of,), jnp.float32, smallest / len(pieces), largest / len(pieces)))
        loudness = loudness * jnp.repeat(draws, shape[dim] // shards_of).reshape([-1 if axis == dim else 1 for axis in range(len(shape))])
    return loudness


def shared_out(key, own, number, rows, amount, top, limit, slope):
    ranking = jax.random.permutation(key, amount)
    heavy_load, common = shares(amount, rows * top, limit, slope, True), shares(amount, rows * top, limit, slope, False)
    places = jnp.arange(amount)

    def named(sizes, offset_by):
        used = int((sizes > 0).sum())
        fixed = max(1, used // 4)
        shifted = fixed + (places - fixed + offset_by * (used - fixed)) % max(1, amount - fixed)
        return jnp.zeros((amount,), jnp.int32).at[ranking[jnp.where(places < fixed, places, shifted)]].set(jnp.asarray(sizes, jnp.int32))

    sizes = jnp.where(number % 4 == 0, named(heavy_load, number // 4), named(common, number - number // 4 - 1))
    mixed = jax.random.permutation(jax.random.fold_in(own, 3), amount)
    donor, taker = mixed[0:amount // 2 * 2:2], mixed[1:amount // 2 * 2:2]
    room = jnp.minimum(sizes[donor] - 1, limit - sizes[taker]) // 2
    room = jnp.where((donor == ranking[0]) | (taker == ranking[0]) | (sizes[taker] == 0), 0, jnp.maximum(room, 0))
    shifted = jax.random.randint(jax.random.fold_in(own, 4), (amount // 2,), 0, 1 << 20) % (room + 1)
    sizes = sizes.at[donor].add(-shifted).at[taker].add(shifted)
    labels = jnp.searchsorted(jnp.cumsum(sizes), jnp.arange(rows * top), side="right").astype(jnp.int32)
    listing = labels.reshape(top, rows).T
    listing = listing[jax.random.permutation(jax.random.fold_in(own, 1), rows)]
    offset_by = jax.random.randint(jax.random.fold_in(own, 2), (rows, 1), 0, top)
    return jnp.take_along_axis(listing, (jnp.arange(top)[None, :] + offset_by) % top, axis=1)


def shares(number_of, total, limit, slope, full):
    portions = [(1 << 20) // math.isqrt(rank ** slope) + 1 for rank in range(1, number_of + 1)]
    largest = limit if full else min(limit, max(-(-total // number_of), total * portions[0] // sum(portions)))
    least = 1 if total - largest >= number_of - 1 else 0
    counts, spare = [largest] + [least] * (number_of - 1), total - largest - least * (number_of - 1)
    while spare > 0:
        candidates = [i for i in range(1, number_of) if counts[i] < largest] or [i for i in range(1, number_of) if counts[i] < limit]
        whole, budget = sum([portions[i] for i in candidates]), spare
        for i in candidates:
            addition = min(limit - counts[i], max(1, budget * portions[i] // whole), spare)
            counts[i] = counts[i] + addition
            spare = spare - addition
    return np.array(counts)


def normal_values(rng, extent, scale, most, cuts=(), kind=jnp.bfloat16):
    level = block_scale(rng, extent, cuts, -0.22, 0.18) if cuts else 1.0
    entries = jax.random.normal(rng, extent, jnp.float32) * scale * level
    return jnp.minimum(jnp.maximum(entries, -most), most).astype(kind)


def setup_inputs(seed: int = 0) -> dict:
    seeds = jax.random.split(jax.random.key(seed), 12)
    item_states = normal_values(seeds[0], (ITEMS, ILEN, DI), 1.0, 6.0, ((0, 128),))
    w_query = normal_values(seeds[1], (DI, DI), DI ** -0.5, 0.125, ((0, 64),))
    w_key = normal_values(seeds[2], (DI, IKV * IHD), DI ** -0.5, 0.125, ((0, 64),))
    w_value = normal_values(seeds[3], (DI, IKV * IHD), DI ** -0.5, 0.125, ((0, 64),))
    item_gain = jnp.clip(1.0 + 0.15 * jax.random.normal(seeds[4], (DI,), jnp.float32), 0.25, 1.75)
    w_adapt = normal_values(seeds[5], (DI, DU), DI ** -0.5, 0.125, ((0, 64),))
    user_gain = jnp.clip(1.0 + 0.15 * jax.random.normal(seeds[6], (DU,), jnp.float32), 0.25, 1.75)
    user_query = normal_values(seeds[7], (DU, UHD), UHD ** -0.5, 0.5, ((0, 64),))
    hist_owner_keys = jax.random.split(jax.random.fold_in(seeds[8], 1), SEQS * LEN // LEN)
    hist_owner_turns = jax.random.permutation(jax.random.fold_in(seeds[8], 3), SEQS * LEN // LEN)
    hist_owner = jax.vmap(lambda own, number: shared_out(jax.random.fold_in(seeds[8], 2), own, number, LEN, DEVICES, 1, CAP, 2))(hist_owner_keys, hist_owner_turns).reshape((SEQS, LEN, 1))
    history_position_index = with_ends(jax.random.randint(seeds[9], (SEQS, LEN), 0, ITEMS_DEV), jax.random.fold_in(seeds[9], 1), 0, ITEMS_DEV - 1).astype(jnp.int32)
    cotangent = normal_values(seeds[10], (SEQS, LEN, DU), 1.0, 6.0, ((0, 128),))
    return dict(item_states=item_states, w_query=w_query, w_key=w_key, w_value=w_value, item_gain=item_gain, w_adapt=w_adapt, user_gain=user_gain, user_query=user_query, hist_owner=hist_owner, history_position_index=history_position_index, cotangent=cotangent)


def stored(values):
    return lax.optimization_barrier(values.astype(jnp.bfloat16))

def rms_scale(values, gain):
    mean_sq = lax.optimization_barrier(jnp.mean(values * values, axis=-1, keepdims=True))
    return values * lax.rsqrt(mean_sq + 1e-05) * gain

def item_pool(states, key_rows, value_rows, query_rows, item_gain):
    count = states.shape[0]
    group = IHEADS // IKV
    query_heads = query_rows.reshape(count, IKV, group, IHD).astype(jnp.float32)
    key_heads = key_rows.reshape(count, ILEN, IKV, IHD).astype(jnp.float32)
    value_heads = value_rows.reshape(count, ILEN, IKV, IHD).astype(jnp.float32)
    scores = jnp.einsum('igrd,itgd->igrt', query_heads, key_heads) * IHD ** (-0.5)
    weights = stored(jax.nn.softmax(scores, axis=-1)).astype(jnp.float32)
    mixed = jnp.einsum('igrt,itgd->igrd', weights, value_heads).reshape(count, IHEADS * IHD)
    last_row = states[:, ILEN - 1, :].astype(jnp.float32)
    return rms_scale(last_row + mixed, item_gain).astype(jnp.bfloat16)

def user_layer(hidden, user_gain, user_query):
    length_total = hidden.shape[0]
    normed = stored(rms_scale(hidden.astype(jnp.float32), user_gain)).astype(jnp.float32)
    heads = normed.reshape(length_total, UHEADS, UHD)
    query_map = user_query.reshape(UHEADS, UHD, UHD).astype(jnp.float32)
    queries = stored(jnp.einsum('thd,hde->the', heads, query_map)).astype(jnp.float32)
    scores = jnp.einsum('the,she->hts', queries, heads) * UHD ** (-0.5)
    target = jnp.arange(length_total, dtype=jnp.int32)
    causal = target[None, :, None] >= target[None, None, :]
    scores = jnp.where(causal, scores, -1e+30)
    weights = stored(jax.nn.softmax(scores, axis=-1)).astype(jnp.float32)
    mixed = jnp.einsum('hts,shd->thd', weights, heads).reshape(length_total, UHEADS * UHD)
    return (hidden.astype(jnp.float32) + mixed).astype(jnp.bfloat16)

def reference(item_states, w_query, w_key, w_value, item_gain, w_adapt, user_gain, user_query, hist_owner, history_position_index, cotangent):
    devices = N_GRP * N_FSDP
    blocks = item_states.reshape(devices, ITEMS_DEV, ILEN, DI)

    def encode(states):
        flat = states.reshape(ITEMS_DEV * ILEN, DI)
        key_rows = stored(jnp.dot(flat, w_key, preferred_element_type=jnp.float32))
        value_rows = stored(jnp.dot(flat, w_value, preferred_element_type=jnp.float32))
        query_rows = stored(jnp.dot(states[:, ILEN - 1, :], w_query, preferred_element_type=jnp.float32))
        return item_pool(states, key_rows, value_rows, query_rows, item_gain)
    item_embed = lax.map(encode, blocks).reshape(ITEMS, DI)
    item_ids = (hist_owner[:, :, 0] * ITEMS_DEV + history_position_index).astype(jnp.int32)

    def user_step(packed):
        ids, grad_out = packed
        fetched = jnp.take(item_embed, ids, axis=0)
        hidden = stored(jnp.dot(fetched, w_adapt, preferred_element_type=jnp.float32))
        result, pull = jax.vjp(lambda values: user_layer(values, user_gain, user_query), hidden)
        grad_hidden, = pull(grad_out)
        grad_rows = jnp.dot(grad_hidden, w_adapt.T, preferred_element_type=jnp.float32)
        return (result, grad_rows)
    user_attention_output, grad_rows = lax.map(user_step, (item_ids, cotangent))
    item_grad = jax.ops.segment_sum(grad_rows.reshape(-1, DI), item_ids.reshape(-1), num_segments=ITEMS)
    return (item_embed, user_attention_output, item_grad)
```

```python
import jax
import jax.numpy as jnp
from jax import lax
from jax.sharding import PartitionSpec as P

DI = 2048
IHEADS = 32
IHD = 64
IKV = 4
UHEADS = 32
UHD = 128
ILEN = 256


def stored(values):
    return lax.optimization_barrier(values.astype(jnp.bfloat16))


def rms_scale(values, gain):
    mean_sq = jnp.mean(values * values, axis=-1, keepdims=True)
    return values * lax.rsqrt(mean_sq + 1e-05) * gain


def item_pool(states, key_rows, value_rows, query_rows, item_gain):
    count = states.shape[0]
    group = IHEADS // IKV
    query_heads = query_rows.reshape(count, IKV, group, IHD).astype(jnp.float32)
    key_heads = key_rows.reshape(count, ILEN, IKV, IHD).astype(jnp.float32)
    value_heads = value_rows.reshape(count, ILEN, IKV, IHD).astype(jnp.float32)
    scores = jnp.einsum("igrd,itgd->igrt", query_heads, key_heads) * IHD ** (-0.5)
    weights = stored(jax.nn.softmax(scores, axis=-1)).astype(jnp.float32)
    mixed = jnp.einsum("igrt,itgd->igrd", weights, value_heads).reshape(count, IHEADS * IHD)
    last_row = states[:, ILEN - 1, :].astype(jnp.float32)
    return rms_scale(last_row + mixed, item_gain).astype(jnp.bfloat16)


def user_layer(hidden, user_gain, user_query):
    length_total = hidden.shape[0]
    normed = stored(rms_scale(hidden.astype(jnp.float32), user_gain)).astype(jnp.float32)
    heads = normed.reshape(length_total, UHEADS, UHD)
    query_map = user_query.reshape(UHEADS, UHD, UHD).astype(jnp.float32)
    queries = stored(jnp.einsum("thd,hde->the", heads, query_map)).astype(jnp.float32)
    scores = jnp.einsum("the,she->hts", queries, heads) * UHD ** (-0.5)
    target = jnp.arange(length_total, dtype=jnp.int32)
    causal = target[None, :, None] >= target[None, None, :]
    scores = jnp.where(causal, scores, -1e30)
    weights = stored(jax.nn.softmax(scores, axis=-1)).astype(jnp.float32)
    mixed = jnp.einsum("hts,shd->thd", weights, heads).reshape(length_total, UHEADS * UHD)
    return (hidden.astype(jnp.float32) + mixed).astype(jnp.bfloat16)


def serve_rows(requests, lookup_matrix):
    chosen_items = (
        requests[..., None] == jnp.arange(lookup_matrix.shape[0], dtype=jnp.int32)
    ).astype(lookup_matrix.dtype)
    return jnp.einsum(
        "ltj,jy->lty", chosen_items, lookup_matrix, preferred_element_type=jnp.float32
    ).astype(lookup_matrix.dtype)


def per_device(
    item_states,
    w_query,
    w_key,
    w_value,
    item_gain,
    w_adapt,
    user_gain,
    user_query,
    hist_owner,
    history_position_index,
    cotangent,
):
    groups = lax.axis_size("grp")
    shards = lax.axis_size("fsdp")
    devices = groups * shards
    count = item_states.shape[0]
    flat = item_states.reshape(count * ILEN, DI)
    last_row = item_states[:, ILEN - 1, :]
    packed = jnp.concatenate(
        [w_key, w_value, w_query, w_adapt, user_query.reshape(w_key.shape[0], -1)], axis=1
    )
    gathered = lax.all_gather(packed, "fsdp", axis=0, tiled=True)
    kv_cols = w_key.shape[1] + w_value.shape[1]
    q_end = kv_cols + w_query.shape[1]
    a_end = q_end + w_adapt.shape[1]
    kv_sum = jnp.dot(flat, gathered[:, :kv_cols], preferred_element_type=jnp.float32)
    key_sum = kv_sum[:, : w_key.shape[1]]
    summed_value = kv_sum[:, w_key.shape[1] :]
    query_sum = jnp.dot(
        last_row, gathered[:, kv_cols:q_end], preferred_element_type=jnp.float32
    )
    adapter = gathered[:, q_end:a_end]
    query_map = gathered[:, a_end:].reshape(-1, user_query.shape[1])
    item_embed = item_pool(
        item_states, stored(key_sum), stored(summed_value), stored(query_sum), item_gain
    )
    length_total = history_position_index.shape[1]
    cap_slots = max(2, 2 * length_total // devices)
    owner_users = hist_owner[0, :, 0]
    owner_hot = (owner_users[:, None] == jnp.arange(devices, dtype=jnp.int32)[None, :]).astype(
        jnp.int32
    )
    earlier = jnp.cumsum(owner_hot, axis=0) - owner_hot
    rank_in = jnp.sum(owner_hot * earlier, axis=1)
    position = owner_users * cap_slots + rank_in
    request = (
        jnp.full((devices * cap_slots,), count, jnp.int32)
        .at[position]
        .set(history_position_index[0])
    )
    request = request.reshape(devices, cap_slots)
    width = item_embed.shape[1]
    incoming = lax.all_to_all(request, ("grp", "fsdp"), split_axis=0, concat_axis=0, tiled=True)
    found = serve_rows(incoming, item_embed)
    returned = lax.all_to_all(found, ("grp", "fsdp"), split_axis=0, concat_axis=0, tiled=True)
    fetched = jnp.take(returned.reshape(devices * cap_slots, width), position, axis=0)
    hidden = stored(jnp.dot(fetched, adapter, preferred_element_type=jnp.float32))
    user_attention_output, pull = jax.vjp(
        lambda values: user_layer(values, user_gain, query_map), hidden
    )
    (grad_hidden,) = pull(cotangent[0])
    grad_rows = jnp.dot(grad_hidden, adapter.T, preferred_element_type=jnp.float32)
    outgoing = jnp.zeros((devices * cap_slots, DI), jnp.float32).at[position].set(grad_rows)
    arrived = lax.all_to_all(
        outgoing.reshape(devices, cap_slots, DI).astype(jnp.bfloat16),
        ("grp", "fsdp"),
        split_axis=0,
        concat_axis=0,
        tiled=True,
    ).astype(jnp.float32)
    terms = arrived.reshape(devices * cap_slots, DI)
    slot_hot = (
        incoming.reshape(-1)[:, None] == jnp.arange(count, dtype=jnp.int32)[None, :]
    ).astype(jnp.float32)
    item_grad = jnp.dot(slot_hot.T, terms, precision=lax.Precision.HIGHEST)
    return (item_embed, user_attention_output[None], item_grad)


def solution(mesh):
    placed = (
        P(("grp", "fsdp"), None, None),
        P("fsdp", None),
        P("fsdp", None),
        P("fsdp", None),
        P(),
        P("fsdp", None),
        P(),
        P("fsdp", None),
        P(("grp", "fsdp"), None, None),
        P(("grp", "fsdp"), None),
        P(("grp", "fsdp"), None, None),
    )
    return jax.shard_map(
        per_device,
        mesh=mesh,
        in_specs=placed,
        out_specs=(
            P(("grp", "fsdp"), None),
            P(("grp", "fsdp"), None, None),
            P(("grp", "fsdp"), None),
        ),
        check_vma=False,
    )
```

```python
import jax
import jax.numpy as jnp
from jax import lax
from jax.sharding import PartitionSpec as P

DI = 2048
IHEADS = 32
IHD = 64
IKV = 4
UHEADS = 32
UHD = 128
ILEN = 256


def stored(values):
    return lax.optimization_barrier(values.astype(jnp.bfloat16))


def rms_scale(values, gain):
    mean_sq = jnp.mean(values * values, axis=-1, keepdims=True)
    return values * lax.rsqrt(mean_sq + 1e-05) * gain


def item_pool(states, key_rows, value_rows, query_rows, item_gain):
    count = states.shape[0]
    group = IHEADS // IKV
    query_heads = query_rows.reshape(count, IKV, group, IHD).astype(jnp.float32)
    key_heads = key_rows.reshape(count, ILEN, IKV, IHD).astype(jnp.float32)
    value_heads = value_rows.reshape(count, ILEN, IKV, IHD).astype(jnp.float32)
    scores = jnp.einsum("igrd,itgd->igrt", query_heads, key_heads) * IHD ** (-0.5)
    weights = stored(jax.nn.softmax(scores, axis=-1)).astype(jnp.float32)
    mixed = jnp.einsum("igrt,itgd->igrd", weights, value_heads).reshape(count, IHEADS * IHD)
    last_row = states[:, ILEN - 1, :].astype(jnp.float32)
    return rms_scale(last_row + mixed, item_gain).astype(jnp.bfloat16)


def user_layer(hidden, user_gain, user_query):
    length_total = hidden.shape[0]
    normed = stored(rms_scale(hidden.astype(jnp.float32), user_gain)).astype(jnp.float32)
    heads = normed.reshape(length_total, UHEADS, UHD)
    query_map = user_query.reshape(UHEADS, UHD, UHD).astype(jnp.float32)
    queries = stored(jnp.einsum("thd,hde->the", heads, query_map)).astype(jnp.float32)
    scores = jnp.einsum("the,she->hts", queries, heads) * UHD ** (-0.5)
    target = jnp.arange(length_total, dtype=jnp.int32)
    causal = target[None, :, None] >= target[None, None, :]
    scores = jnp.where(causal, scores, -1e30)
    weights = stored(jax.nn.softmax(scores, axis=-1)).astype(jnp.float32)
    mixed = jnp.einsum("hts,shd->thd", weights, heads).reshape(length_total, UHEADS * UHD)
    return (hidden.astype(jnp.float32) + mixed).astype(jnp.bfloat16)


def serve_rows(requests, lookup_matrix):
    chosen_items = (
        requests[..., None] == jnp.arange(lookup_matrix.shape[0], dtype=jnp.int32)
    ).astype(lookup_matrix.dtype)
    return jnp.einsum(
        "ltj,jy->lty", chosen_items, lookup_matrix, preferred_element_type=jnp.float32
    ).astype(lookup_matrix.dtype)


def per_device(
    item_states,
    w_query,
    w_key,
    w_value,
    item_gain,
    w_adapt,
    user_gain,
    user_query,
    hist_owner,
    history_position_index,
    cotangent,
):
    groups = lax.axis_size("grp")
    shards = lax.axis_size("fsdp")
    devices = groups * shards
    count = item_states.shape[0]
    flat = item_states.reshape(count * ILEN, DI)
    last_row = item_states[:, ILEN - 1, :]
    side = lax.axis_index("grp")

    def half(w, rows=None):
        w = w if rows is None else w.reshape(rows, -1)
        return lax.dynamic_slice_in_dim(w, side * (w.shape[1] // 2), w.shape[1] // 2, axis=1)

    pieces = [half(w_key), half(w_value), half(w_query), half(w_adapt), half(user_query, w_key.shape[0])]
    widths = [p.shape[1] for p in pieces]
    ends = [sum(widths[: i + 1]) for i in range(len(widths))]
    gathered = lax.all_gather(
        jnp.concatenate(pieces, axis=1), ("grp", "fsdp"), axis=0, tiled=True
    ).reshape(groups, DI, ends[-1])
    kv_sum = jnp.einsum(
        "td,gdc->tgc", flat, gathered[:, :, : ends[1]], preferred_element_type=jnp.float32
    )
    key_sum = kv_sum[:, :, : widths[0]].reshape(flat.shape[0], -1)
    summed_value = kv_sum[:, :, widths[0] :].reshape(flat.shape[0], -1)
    query_sum = jnp.einsum(
        "id,gdc->igc", last_row, gathered[:, :, ends[1] : ends[2]], preferred_element_type=jnp.float32
    ).reshape(count, -1)
    adapter_halves = gathered[:, :, ends[2] : ends[3]]
    query_map = (
        gathered[:, :, ends[3] :]
        .reshape(groups, DI, -1, user_query.shape[1])
        .transpose(1, 2, 0, 3)
        .reshape(-1, user_query.shape[1])
    )
    item_embed = item_pool(
        item_states, stored(key_sum), stored(summed_value), stored(query_sum), item_gain
    )
    length_total = history_position_index.shape[1]
    cap_slots = max(2, 2 * length_total // devices)
    owner_users = hist_owner[0, :, 0]
    owner_hot = (owner_users[:, None] == jnp.arange(devices, dtype=jnp.int32)[None, :]).astype(
        jnp.int32
    )
    earlier = jnp.cumsum(owner_hot, axis=0) - owner_hot
    rank_in = jnp.sum(owner_hot * earlier, axis=1)
    position = owner_users * cap_slots + rank_in
    request = (
        jnp.full((devices * cap_slots,), count, jnp.int32)
        .at[position]
        .set(history_position_index[0])
    )
    request = request.reshape(devices, cap_slots)
    width = item_embed.shape[1]
    incoming = lax.all_to_all(request, ("grp", "fsdp"), split_axis=0, concat_axis=0, tiled=True)
    found = serve_rows(incoming, item_embed)
    returned = lax.all_to_all(found, ("grp", "fsdp"), split_axis=0, concat_axis=0, tiled=True)
    fetched = jnp.take(returned.reshape(devices * cap_slots, width), position, axis=0)
    hidden = stored(
        jnp.einsum("td,gdc->tgc", fetched, adapter_halves, preferred_element_type=jnp.float32).reshape(
            fetched.shape[0], -1
        )
    )
    user_attention_output, pull = jax.vjp(
        lambda values: user_layer(values, user_gain, query_map), hidden
    )
    (grad_hidden,) = pull(cotangent[0])
    grad_rows = jnp.einsum(
        "tgc,gdc->td",
        grad_hidden.reshape(grad_hidden.shape[0], groups, -1),
        adapter_halves,
        preferred_element_type=jnp.float32,
    )
    outgoing = jnp.zeros((devices * cap_slots, DI), jnp.float32).at[position].set(grad_rows)
    arrived = lax.all_to_all(
        outgoing.reshape(devices, cap_slots, DI).astype(jnp.bfloat16),
        ("grp", "fsdp"),
        split_axis=0,
        concat_axis=0,
        tiled=True,
    ).astype(jnp.float32)
    terms = arrived.reshape(devices * cap_slots, DI)
    slot_hot = (
        incoming.reshape(-1)[:, None] == jnp.arange(count, dtype=jnp.int32)[None, :]
    ).astype(jnp.float32)
    item_grad = jnp.dot(slot_hot.T, terms, precision=lax.Precision.HIGHEST)
    return (item_embed, user_attention_output[None], item_grad)


def solution(mesh):
    placed = (
        P(("grp", "fsdp"), None, None),
        P("fsdp", None),
        P("fsdp", None),
        P("fsdp", None),
        P(),
        P("fsdp", None),
        P(),
        P("fsdp", None),
        P(("grp", "fsdp"), None, None),
        P(("grp", "fsdp"), None),
        P(("grp", "fsdp"), None, None),
    )
    return jax.shard_map(
        per_device,
        mesh=mesh,
        in_specs=placed,
        out_specs=(
            P(("grp", "fsdp"), None),
            P(("grp", "fsdp"), None, None),
            P(("grp", "fsdp"), None),
        ),
        check_vma=False,
    )
```

```python
import jax
import jax.numpy as jnp
from jax import lax
from jax.sharding import PartitionSpec as P

DI = 2048
IHEADS = 32
IHD = 64
IKV = 4
UHEADS = 32
UHD = 128
ILEN = 256


def stored(values):
    return lax.optimization_barrier(values.astype(jnp.bfloat16))


def rms_scale(values, gain):
    mean_sq = jnp.mean(values * values, axis=-1, keepdims=True)
    return values * lax.rsqrt(mean_sq + 1e-05) * gain


def item_pool(states, key_rows, value_rows, query_rows, item_gain):
    count = states.shape[0]
    group = IHEADS // IKV
    query_heads = query_rows.reshape(count, IKV, group, IHD).astype(jnp.float32)
    key_heads = key_rows.reshape(count, ILEN, IKV, IHD).astype(jnp.float32)
    value_heads = value_rows.reshape(count, ILEN, IKV, IHD).astype(jnp.float32)
    scores = jnp.einsum("igrd,itgd->igrt", query_heads, key_heads) * IHD ** (-0.5)
    weights = stored(jax.nn.softmax(scores, axis=-1)).astype(jnp.float32)
    mixed = jnp.einsum("igrt,itgd->igrd", weights, value_heads).reshape(count, IHEADS * IHD)
    last_row = states[:, ILEN - 1, :].astype(jnp.float32)
    return rms_scale(last_row + mixed, item_gain).astype(jnp.bfloat16)


def user_layer(hidden, user_gain, user_query):
    length_total = hidden.shape[0]
    normed = stored(rms_scale(hidden.astype(jnp.float32), user_gain)).astype(jnp.float32)
    heads = normed.reshape(length_total, UHEADS, UHD)
    query_map = user_query.reshape(UHEADS, UHD, UHD).astype(jnp.float32)
    queries = stored(jnp.einsum("thd,hde->the", heads, query_map)).astype(jnp.float32)
    scores = jnp.einsum("the,she->hts", queries, heads) * UHD ** (-0.5)
    target = jnp.arange(length_total, dtype=jnp.int32)
    causal = target[None, :, None] >= target[None, None, :]
    scores = jnp.where(causal, scores, -1e30)
    weights = stored(jax.nn.softmax(scores, axis=-1)).astype(jnp.float32)
    mixed = jnp.einsum("hts,shd->thd", weights, heads).reshape(length_total, UHEADS * UHD)
    return (hidden.astype(jnp.float32) + mixed).astype(jnp.bfloat16)


def serve_rows(requests, lookup_matrix):
    chosen_items = (
        requests[..., None] == jnp.arange(lookup_matrix.shape[0], dtype=jnp.int32)
    ).astype(lookup_matrix.dtype)
    return jnp.einsum(
        "ltj,jy->lty", chosen_items, lookup_matrix, preferred_element_type=jnp.float32
    ).astype(lookup_matrix.dtype)


def per_device(
    item_states,
    w_query,
    w_key,
    w_value,
    item_gain,
    w_adapt,
    user_gain,
    user_query,
    hist_owner,
    history_position_index,
    cotangent,
):
    groups = lax.axis_size("grp")
    shards = lax.axis_size("fsdp")
    devices = groups * shards
    count = item_states.shape[0]
    flat = item_states.reshape(count * ILEN, DI)
    last_row = item_states[:, ILEN - 1, :]
    side = lax.axis_index("grp")
    query_rows_of = user_query.reshape(w_key.shape[0], -1)

    def halves(w):
        return [w[:, i * (w.shape[1] // groups) : (i + 1) * (w.shape[1] // groups)] for i in range(groups)]

    split = [halves(w) for w in (w_adapt, w_query, w_key, w_value)]
    widths = [part[0].shape[1] for part in split] + [query_rows_of.shape[1]]
    ends = [sum(widths[: i + 1]) for i in range(len(widths))]
    both = jnp.concatenate(
        [piece for i in range(groups) for piece in [part[i] for part in split] + [query_rows_of]], axis=1
    )
    gathered = lax.all_gather(
        lax.dynamic_slice_in_dim(both, side * ends[-1], ends[-1], axis=1),
        ("grp", "fsdp"),
        axis=0,
        tiled=True,
    ).reshape(groups, DI, ends[-1])
    kv_sum = jnp.einsum(
        "td,gdc->tgc", flat, gathered[:, :, ends[1] : ends[3]], preferred_element_type=jnp.float32
    )
    key_sum = kv_sum[:, :, : widths[2]].reshape(flat.shape[0], -1)
    summed_value = kv_sum[:, :, widths[2] :].reshape(flat.shape[0], -1)
    query_sum = jnp.einsum(
        "id,gdc->igc", last_row, gathered[:, :, ends[0] : ends[1]], preferred_element_type=jnp.float32
    ).reshape(count, -1)
    adapter_halves = gathered[:, :, : ends[0]]
    query_map = gathered[0, :, ends[3] :].reshape(-1, user_query.shape[1])
    item_embed = item_pool(
        item_states, stored(key_sum), stored(summed_value), stored(query_sum), item_gain
    )
    length_total = history_position_index.shape[1]
    cap_slots = max(2, 2 * length_total // devices)
    owner_users = hist_owner[0, :, 0]
    owner_hot = (owner_users[:, None] == jnp.arange(devices, dtype=jnp.int32)[None, :]).astype(
        jnp.int32
    )
    earlier = jnp.cumsum(owner_hot, axis=0) - owner_hot
    rank_in = jnp.sum(owner_hot * earlier, axis=1)
    position = owner_users * cap_slots + rank_in
    request = (
        jnp.full((devices * cap_slots,), count, jnp.int32)
        .at[position]
        .set(history_position_index[0])
    )
    request = request.reshape(devices, cap_slots)
    width = item_embed.shape[1]
    incoming = lax.all_to_all(request, ("grp", "fsdp"), split_axis=0, concat_axis=0, tiled=True)
    found = serve_rows(incoming, item_embed)
    returned = lax.all_to_all(found, ("grp", "fsdp"), split_axis=0, concat_axis=0, tiled=True)
    fetched = jnp.take(returned.reshape(devices * cap_slots, width), position, axis=0)
    hidden = stored(
        jnp.einsum("td,gdc->tgc", fetched, adapter_halves, preferred_element_type=jnp.float32).reshape(
            fetched.shape[0], -1
        )
    )
    user_attention_output, pull = jax.vjp(
        lambda values: user_layer(values, user_gain, query_map), hidden
    )
    (grad_hidden,) = pull(cotangent[0])
    grad_rows = jnp.einsum(
        "tgc,gdc->td",
        grad_hidden.reshape(grad_hidden.shape[0], groups, -1),
        adapter_halves,
        preferred_element_type=jnp.float32,
    )
    outgoing = jnp.zeros((devices * cap_slots, DI), jnp.float32).at[position].set(grad_rows)
    arrived = lax.all_to_all(
        outgoing.reshape(devices, cap_slots, DI).astype(jnp.bfloat16),
        ("grp", "fsdp"),
        split_axis=0,
        concat_axis=0,
        tiled=True,
    ).astype(jnp.float32)
    terms = arrived.reshape(devices * cap_slots, DI)
    slot_hot = (
        incoming.reshape(-1)[:, None] == jnp.arange(count, dtype=jnp.int32)[None, :]
    ).astype(jnp.float32)
    item_grad = jnp.dot(slot_hot.T, terms, precision=lax.Precision.HIGHEST)
    return (item_embed, user_attention_output[None], item_grad)


def solution(mesh):
    placed = (
        P(("grp", "fsdp"), None, None),
        P("fsdp", None),
        P("fsdp", None),
        P("fsdp", None),
        P(),
        P("fsdp", None),
        P(),
        P("fsdp", None),
        P(("grp", "fsdp"), None, None),
        P(("grp", "fsdp"), None),
        P(("grp", "fsdp"), None, None),
    )
    return jax.shard_map(
        per_device,
        mesh=mesh,
        in_specs=placed,
        out_specs=(
            P(("grp", "fsdp"), None),
            P(("grp", "fsdp"), None, None),
            P(("grp", "fsdp"), None),
        ),
        check_vma=False,
    )
```

```python
import jax
import jax.numpy as jnp
from jax import lax
from jax.sharding import PartitionSpec as P

DI = 2048
IHEADS = 32
IHD = 64
IKV = 4
UHEADS = 32
UHD = 128
ILEN = 256


def stored(values):
    return lax.optimization_barrier(values.astype(jnp.bfloat16))


def rms_scale(values, gain):
    mean_sq = jnp.mean(values * values, axis=-1, keepdims=True)
    return values * lax.rsqrt(mean_sq + 1e-05) * gain


def item_pool(states, key_rows, value_rows, query_rows, item_gain):
    count = states.shape[0]
    group = IHEADS // IKV
    query_heads = query_rows.reshape(count, IKV, group, IHD).astype(jnp.float32)
    key_heads = key_rows.reshape(count, ILEN, IKV, IHD).astype(jnp.float32)
    value_heads = value_rows.reshape(count, ILEN, IKV, IHD).astype(jnp.float32)
    scores = jnp.einsum("igrd,itgd->igrt", query_heads, key_heads) * IHD ** (-0.5)
    weights = stored(jax.nn.softmax(scores, axis=-1)).astype(jnp.float32)
    mixed = jnp.einsum("igrt,itgd->igrd", weights, value_heads).reshape(count, IHEADS * IHD)
    last_row = states[:, ILEN - 1, :].astype(jnp.float32)
    return rms_scale(last_row + mixed, item_gain).astype(jnp.bfloat16)


def user_layer(hidden, user_gain, user_query):
    length_total = hidden.shape[0]
    normed = stored(rms_scale(hidden.astype(jnp.float32), user_gain)).astype(jnp.float32)
    heads = normed.reshape(length_total, UHEADS, UHD)
    query_map = user_query.reshape(UHEADS, UHD, UHD).astype(jnp.float32)
    queries = stored(jnp.einsum("thd,hde->the", heads, query_map)).astype(jnp.float32)
    scores = jnp.einsum("the,she->hts", queries, heads) * UHD ** (-0.5)
    target = jnp.arange(length_total, dtype=jnp.int32)
    causal = target[None, :, None] >= target[None, None, :]
    scores = jnp.where(causal, scores, -1e30)
    weights = stored(jax.nn.softmax(scores, axis=-1)).astype(jnp.float32)
    mixed = jnp.einsum("hts,shd->thd", weights, heads).reshape(length_total, UHEADS * UHD)
    return (hidden.astype(jnp.float32) + mixed).astype(jnp.bfloat16)


def serve_rows(requests, lookup_matrix):
    chosen_items = (
        requests[..., None] == jnp.arange(lookup_matrix.shape[0], dtype=jnp.int32)
    ).astype(lookup_matrix.dtype)
    return jnp.einsum(
        "ltj,jy->lty", chosen_items, lookup_matrix, preferred_element_type=jnp.float32
    ).astype(lookup_matrix.dtype)


def per_device(
    item_states,
    w_query,
    w_key,
    w_value,
    item_gain,
    w_adapt,
    user_gain,
    user_query,
    hist_owner,
    history_position_index,
    cotangent,
):
    groups = lax.axis_size("grp")
    shards = lax.axis_size("fsdp")
    devices = groups * shards
    count = item_states.shape[0]
    flat = item_states.reshape(count * ILEN, DI)
    last_row = item_states[:, ILEN - 1, :]
    side = lax.axis_index("grp")

    def half(w, rows=None):
        w = w if rows is None else w.reshape(rows, -1)
        return lax.dynamic_slice_in_dim(w, side * (w.shape[1] // 2), w.shape[1] // 2, axis=1)

    pieces = [half(w_key), half(w_value), half(w_query), half(w_adapt), half(user_query, w_key.shape[0])]
    widths = [p.shape[1] for p in pieces]
    ends = [sum(widths[: i + 1]) for i in range(len(widths))]
    gathered = lax.all_gather(
        jnp.concatenate(pieces, axis=1), ("grp", "fsdp"), axis=0, tiled=True
    ).reshape(groups, DI, ends[-1])
    kv_sum = jnp.einsum(
        "td,gdc->tgc", flat, gathered[:, :, : ends[1]], preferred_element_type=jnp.float32
    )
    key_sum = kv_sum[:, :, : widths[0]].reshape(flat.shape[0], -1)
    summed_value = kv_sum[:, :, widths[0] :].reshape(flat.shape[0], -1)
    query_sum = jnp.einsum(
        "id,gdc->igc", last_row, gathered[:, :, ends[1] : ends[2]], preferred_element_type=jnp.float32
    ).reshape(count, -1)
    adapter_halves = gathered[:, :, ends[2] : ends[3]]
    query_map = (
        gathered[:, :, ends[3] :]
        .reshape(groups, DI, -1, user_query.shape[1])
        .transpose(1, 2, 0, 3)
        .reshape(-1, user_query.shape[1])
    )
    item_embed = item_pool(
        item_states, stored(key_sum), stored(summed_value), stored(query_sum), item_gain
    )
    length_total = history_position_index.shape[1]
    cap_slots = max(2, 2 * length_total // devices)
    owner_users = hist_owner[0, :, 0]
    owner_hot = (owner_users[:, None] == jnp.arange(devices, dtype=jnp.int32)[None, :]).astype(
        jnp.int32
    )
    earlier = jnp.cumsum(owner_hot, axis=0) - owner_hot
    rank_in = jnp.sum(owner_hot * earlier, axis=1)
    position = owner_users * cap_slots + rank_in
    request = (
        jnp.full((devices * cap_slots,), count, jnp.int32)
        .at[position]
        .set(history_position_index[0])
    )
    request = request.reshape(devices, cap_slots)
    width = item_embed.shape[1]
    incoming = lax.all_to_all(request, ("grp", "fsdp"), split_axis=0, concat_axis=0, tiled=True)
    found = serve_rows(incoming, item_embed)
    returned = lax.all_to_all(found, ("grp", "fsdp"), split_axis=0, concat_axis=0, tiled=True)
    fetched = jnp.take(returned.reshape(devices * cap_slots, width), position, axis=0)
    hidden = stored(
        jnp.einsum("td,gdc->tgc", fetched, adapter_halves, preferred_element_type=jnp.float32).reshape(
            fetched.shape[0], -1
        )
    )
    user_attention_output, pull = jax.vjp(
        lambda values: user_layer(values, user_gain, query_map), hidden
    )
    (grad_hidden,) = pull(cotangent[0])
    slot_of = (
        position[None, :] == jnp.arange(devices * cap_slots, dtype=jnp.int32)[:, None]
    ).astype(grad_hidden.dtype)
    slot_grads = jnp.dot(slot_of, grad_hidden, preferred_element_type=jnp.float32).astype(
        grad_hidden.dtype
    )
    outgoing = jnp.einsum(
        "tgc,gdc->td",
        slot_grads.reshape(slot_grads.shape[0], groups, -1),
        adapter_halves,
        preferred_element_type=jnp.float32,
    ).astype(jnp.bfloat16)
    arrived = lax.all_to_all(
        outgoing.reshape(devices, cap_slots, DI),
        ("grp", "fsdp"),
        split_axis=0,
        concat_axis=0,
        tiled=True,
    ).astype(jnp.float32)
    terms = arrived.reshape(devices * cap_slots, DI)
    slot_hot = (
        incoming.reshape(-1)[:, None] == jnp.arange(count, dtype=jnp.int32)[None, :]
    ).astype(jnp.float32)
    item_grad = jnp.dot(slot_hot.T, terms, precision=lax.Precision.HIGHEST)
    return (item_embed, user_attention_output[None], item_grad)


def solution(mesh):
    placed = (
        P(("grp", "fsdp"), None, None),
        P("fsdp", None),
        P("fsdp", None),
        P("fsdp", None),
        P(),
        P("fsdp", None),
        P(),
        P("fsdp", None),
        P(("grp", "fsdp"), None, None),
        P(("grp", "fsdp"), None),
        P(("grp", "fsdp"), None, None),
    )
    return jax.shard_map(
        per_device,
        mesh=mesh,
        in_specs=placed,
        out_specs=(
            P(("grp", "fsdp"), None),
            P(("grp", "fsdp"), None, None),
            P(("grp", "fsdp"), None),
        ),
        check_vma=False,
    )
```

```python
import jax
import jax.numpy as jnp
from jax import lax
from jax.experimental import pallas as pl
from jax.experimental.pallas import tpu as pltpu
from jax.sharding import PartitionSpec as P

DI = 2048
IHEADS = 32
IHD = 64
IKV = 4
UHEADS = 32
UHD = 128
ILEN = 256


def stored(values):
    return lax.optimization_barrier(values.astype(jnp.bfloat16))


def rms_scale(values, gain):
    mean_sq = jnp.mean(values * values, axis=-1, keepdims=True)
    return values * lax.rsqrt(mean_sq + 1e-05) * gain


def item_pool(states, key_rows, value_rows, query_rows, item_gain):
    count = states.shape[0]
    group = IHEADS // IKV
    query_heads = query_rows.reshape(count, IKV, group, IHD).astype(jnp.float32)
    key_heads = key_rows.reshape(count, ILEN, IKV, IHD).astype(jnp.float32)
    value_heads = value_rows.reshape(count, ILEN, IKV, IHD).astype(jnp.float32)
    scores = jnp.einsum("igrd,itgd->igrt", query_heads, key_heads) * IHD ** (-0.5)
    weights = stored(jax.nn.softmax(scores, axis=-1)).astype(jnp.float32)
    mixed = jnp.einsum("igrt,itgd->igrd", weights, value_heads).reshape(count, IHEADS * IHD)
    last_row = states[:, ILEN - 1, :].astype(jnp.float32)
    return rms_scale(last_row + mixed, item_gain).astype(jnp.bfloat16)


def user_layer(hidden, user_gain, user_query):
    length_total = hidden.shape[0]
    normed = stored(rms_scale(hidden.astype(jnp.float32), user_gain)).astype(jnp.float32)
    heads = normed.reshape(length_total, UHEADS, UHD)
    query_map = user_query.reshape(UHEADS, UHD, UHD).astype(jnp.float32)
    queries = stored(jnp.einsum("thd,hde->the", heads, query_map)).astype(jnp.float32)
    scores = jnp.einsum("the,she->hts", queries, heads) * UHD ** (-0.5)
    target = jnp.arange(length_total, dtype=jnp.int32)
    causal = target[None, :, None] >= target[None, None, :]
    scores = jnp.where(causal, scores, -1e30)
    weights = stored(jax.nn.softmax(scores, axis=-1)).astype(jnp.float32)
    mixed = jnp.einsum("hts,shd->thd", weights, heads).reshape(length_total, UHEADS * UHD)
    return (hidden.astype(jnp.float32) + mixed).astype(jnp.bfloat16)


def _pack_halves(*refs):
    sources, out, sems = refs[:-2], refs[-2], refs[-1]
    side = lax.axis_index("grp")
    copies, column = [], 0
    for i, src in enumerate(sources):
        if i == len(sources) - 1:
            rows = src.shape[0] // 2
            width = src.shape[1]
            window = src.at[pl.ds(side * rows, rows), :]
        else:
            width = src.shape[1] // 2
            window = src.at[:, pl.ds(side * width, width)]
        copy = pltpu.make_async_copy(window, out.at[:, pl.ds(column, width)], sems.at[i])
        copy.start()
        copies.append(copy)
        column += width
    for copy in copies:
        copy.wait()


def pack_halves(sources):
    total = sum(w.shape[1] // 2 for w in sources[:-1]) + sources[-1].shape[1]
    return pl.pallas_call(
        _pack_halves,
        out_shape=jax.ShapeDtypeStruct((sources[0].shape[0], total), sources[0].dtype),
        in_specs=[pl.BlockSpec(memory_space=pl.ANY)] * len(sources),
        out_specs=pl.BlockSpec(memory_space=pl.ANY),
        scratch_shapes=[pltpu.SemaphoreType.DMA((len(sources),))],
    )(*sources)


def serve_rows(requests, lookup_matrix):
    chosen_items = (
        requests[..., None] == jnp.arange(lookup_matrix.shape[0], dtype=jnp.int32)
    ).astype(lookup_matrix.dtype)
    return jnp.einsum(
        "ltj,jy->lty", chosen_items, lookup_matrix, preferred_element_type=jnp.float32
    ).astype(lookup_matrix.dtype)


def per_device(
    item_states,
    w_query,
    w_key,
    w_value,
    item_gain,
    w_adapt,
    user_gain,
    user_query,
    hist_owner,
    history_position_index,
    cotangent,
):
    groups = lax.axis_size("grp")
    shards = lax.axis_size("fsdp")
    devices = groups * shards
    count = item_states.shape[0]
    flat = item_states.reshape(count * ILEN, DI)
    last_row = item_states[:, ILEN - 1, :]
    side = lax.axis_index("grp")

    sources = [w_key, w_value, w_query, w_adapt, user_query]
    widths = [w.shape[1] // 2 for w in sources[:-1]] + [user_query.shape[1]]
    ends = [sum(widths[: i + 1]) for i in range(len(widths))]
    gathered = lax.all_gather(
        pack_halves(sources), ("grp", "fsdp"), axis=0, tiled=True
    ).reshape(groups, DI, ends[-1])
    kv_sum = jnp.einsum(
        "td,gdc->tgc", flat, gathered[:, :, : ends[1]], preferred_element_type=jnp.float32
    )
    key_sum = kv_sum[:, :, : widths[0]].reshape(flat.shape[0], -1)
    summed_value = kv_sum[:, :, widths[0] :].reshape(flat.shape[0], -1)
    query_sum = jnp.einsum(
        "id,gdc->igc", last_row, gathered[:, :, ends[1] : ends[2]], preferred_element_type=jnp.float32
    ).reshape(count, -1)
    adapter_halves = gathered[:, :, ends[2] : ends[3]]
    query_map = (
        gathered[:, :, ends[3] :]
        .reshape(groups, shards, -1, user_query.shape[1])
        .transpose(1, 0, 2, 3)
        .reshape(-1, user_query.shape[1])
    )
    item_embed = item_pool(
        item_states, stored(key_sum), stored(summed_value), stored(query_sum), item_gain
    )
    length_total = history_position_index.shape[1]
    cap_slots = max(2, 2 * length_total // devices)
    owner_users = hist_owner[0, :, 0]
    owner_hot = (owner_users[:, None] == jnp.arange(devices, dtype=jnp.int32)[None, :]).astype(
        jnp.int32
    )
    earlier = jnp.cumsum(owner_hot, axis=0) - owner_hot
    rank_in = jnp.sum(owner_hot * earlier, axis=1)
    position = owner_users * cap_slots + rank_in
    request = (
        jnp.full((devices * cap_slots,), count, jnp.int32)
        .at[position]
        .set(history_position_index[0])
    )
    request = request.reshape(devices, cap_slots)
    width = item_embed.shape[1]
    incoming = lax.all_to_all(request, ("grp", "fsdp"), split_axis=0, concat_axis=0, tiled=True)
    found = serve_rows(incoming, item_embed)
    returned = lax.all_to_all(found, ("grp", "fsdp"), split_axis=0, concat_axis=0, tiled=True)
    fetched = jnp.take(returned.reshape(devices * cap_slots, width), position, axis=0)
    hidden = stored(
        jnp.einsum("td,gdc->tgc", fetched, adapter_halves, preferred_element_type=jnp.float32).reshape(
            fetched.shape[0], -1
        )
    )
    user_attention_output, pull = jax.vjp(
        lambda values: user_layer(values, user_gain, query_map), hidden
    )
    (grad_hidden,) = pull(cotangent[0])
    slot_of = (
        position[None, :] == jnp.arange(devices * cap_slots, dtype=jnp.int32)[:, None]
    ).astype(grad_hidden.dtype)
    slot_grads = jnp.dot(slot_of, grad_hidden, preferred_element_type=jnp.float32).astype(
        grad_hidden.dtype
    )
    outgoing = jnp.einsum(
        "tgc,gdc->td",
        slot_grads.reshape(slot_grads.shape[0], groups, -1),
        adapter_halves,
        preferred_element_type=jnp.float32,
    ).astype(jnp.bfloat16)
    arrived = lax.all_to_all(
        outgoing.reshape(devices, cap_slots, DI),
        ("grp", "fsdp"),
        split_axis=0,
        concat_axis=0,
        tiled=True,
    ).astype(jnp.float32)
    terms = arrived.reshape(devices * cap_slots, DI)
    slot_hot = (
        incoming.reshape(-1)[:, None] == jnp.arange(count, dtype=jnp.int32)[None, :]
    ).astype(jnp.float32)
    item_grad = jnp.dot(slot_hot.T, terms, precision=lax.Precision.HIGHEST)
    return (item_embed, user_attention_output[None], item_grad)


def solution(mesh):
    placed = (
        P(("grp", "fsdp"), None, None),
        P("fsdp", None),
        P("fsdp", None),
        P("fsdp", None),
        P(),
        P("fsdp", None),
        P(),
        P("fsdp", None),
        P(("grp", "fsdp"), None, None),
        P(("grp", "fsdp"), None),
        P(("grp", "fsdp"), None, None),
    )
    return jax.shard_map(
        per_device,
        mesh=mesh,
        in_specs=placed,
        out_specs=(
            P(("grp", "fsdp"), None),
            P(("grp", "fsdp"), None, None),
            P(("grp", "fsdp"), None),
        ),
        check_vma=False,
    )
```

```python
import jax
import jax.numpy as jnp
from jax import lax
from jax.experimental import pallas as pl
from jax.experimental.pallas import tpu as pltpu
from jax.sharding import PartitionSpec as P

DI = 2048
IHEADS = 32
IHD = 64
IKV = 4
UHEADS = 32
UHD = 128
ILEN = 256


def stored(values):
    return lax.optimization_barrier(values.astype(jnp.bfloat16))


def rms_scale(values, gain):
    mean_sq = jnp.mean(values * values, axis=-1, keepdims=True)
    return values * lax.rsqrt(mean_sq + 1e-05) * gain


def item_pool(states, key_rows, value_rows, query_rows, item_gain):
    count = states.shape[0]
    group = IHEADS // IKV
    query_heads = query_rows.reshape(count, IKV, group, IHD).astype(jnp.float32)
    key_heads = key_rows.reshape(count, ILEN, IKV, IHD).astype(jnp.float32)
    value_heads = value_rows.reshape(count, ILEN, IKV, IHD).astype(jnp.float32)
    scores = jnp.einsum("igrd,itgd->igrt", query_heads, key_heads) * IHD ** (-0.5)
    weights = stored(jax.nn.softmax(scores, axis=-1)).astype(jnp.float32)
    mixed = jnp.einsum("igrt,itgd->igrd", weights, value_heads).reshape(count, IHEADS * IHD)
    last_row = states[:, ILEN - 1, :].astype(jnp.float32)
    return rms_scale(last_row + mixed, item_gain).astype(jnp.bfloat16)


def user_layer(hidden, user_gain, user_query):
    length_total = hidden.shape[0]
    normed = stored(rms_scale(hidden.astype(jnp.float32), user_gain)).astype(jnp.float32)
    heads = normed.reshape(length_total, UHEADS, UHD)
    query_map = user_query.reshape(UHEADS, UHD, UHD).astype(jnp.float32)
    queries = stored(jnp.einsum("thd,hde->the", heads, query_map)).astype(jnp.float32)
    scores = jnp.einsum("the,she->hts", queries, heads) * UHD ** (-0.5)
    target = jnp.arange(length_total, dtype=jnp.int32)
    causal = target[None, :, None] >= target[None, None, :]
    scores = jnp.where(causal, scores, -1e30)
    weights = stored(jax.nn.softmax(scores, axis=-1)).astype(jnp.float32)
    mixed = jnp.einsum("hts,shd->thd", weights, heads).reshape(length_total, UHEADS * UHD)
    return (hidden.astype(jnp.float32) + mixed).astype(jnp.bfloat16)


def _pack_halves(*refs):
    sources, out = refs[:-1], refs[-1]
    first = lax.axis_index("grp") == 0
    column = 0
    for i, src in enumerate(sources):
        if i == len(sources) - 1:
            rows = src.shape[0] // 2
            width = src.shape[1]
            low, high = src[:rows, :], src[rows:, :]
        else:
            width = src.shape[1] // 2
            low, high = src[:, :width], src[:, width:]
        out[:, column : column + width] = jnp.where(first, low, high)
        column += width


def pack_halves(sources):
    total = sum(w.shape[1] // 2 for w in sources[:-1]) + sources[-1].shape[1]
    return pl.pallas_call(
        _pack_halves,
        out_shape=jax.ShapeDtypeStruct((sources[0].shape[0], total), sources[0].dtype),
    )(*sources)


def serve_rows(requests, lookup_matrix):
    chosen_items = (
        requests[..., None] == jnp.arange(lookup_matrix.shape[0], dtype=jnp.int32)
    ).astype(lookup_matrix.dtype)
    return jnp.einsum(
        "ltj,jy->lty", chosen_items, lookup_matrix, preferred_element_type=jnp.float32
    ).astype(lookup_matrix.dtype)


def per_device(
    item_states,
    w_query,
    w_key,
    w_value,
    item_gain,
    w_adapt,
    user_gain,
    user_query,
    hist_owner,
    history_position_index,
    cotangent,
):
    groups = lax.axis_size("grp")
    shards = lax.axis_size("fsdp")
    devices = groups * shards
    count = item_states.shape[0]
    flat = item_states.reshape(count * ILEN, DI)
    last_row = item_states[:, ILEN - 1, :]
    side = lax.axis_index("grp")

    sources = [w_key, w_value, w_query, w_adapt, user_query]
    widths = [w.shape[1] // 2 for w in sources[:-1]] + [user_query.shape[1]]
    ends = [sum(widths[: i + 1]) for i in range(len(widths))]
    gathered = lax.all_gather(
        pack_halves(sources), ("grp", "fsdp"), axis=0, tiled=True
    ).reshape(groups, DI, ends[-1])
    kv_sum = jnp.einsum(
        "td,gdc->tgc", flat, gathered[:, :, : ends[1]], preferred_element_type=jnp.float32
    )
    key_sum = kv_sum[:, :, : widths[0]].reshape(flat.shape[0], -1)
    summed_value = kv_sum[:, :, widths[0] :].reshape(flat.shape[0], -1)
    query_sum = jnp.einsum(
        "id,gdc->igc", last_row, gathered[:, :, ends[1] : ends[2]], preferred_element_type=jnp.float32
    ).reshape(count, -1)
    adapter_halves = gathered[:, :, ends[2] : ends[3]]
    query_map = (
        gathered[:, :, ends[3] :]
        .reshape(groups, shards, -1, user_query.shape[1])
        .transpose(1, 0, 2, 3)
        .reshape(-1, user_query.shape[1])
    )
    item_embed = item_pool(
        item_states, stored(key_sum), stored(summed_value), stored(query_sum), item_gain
    )
    length_total = history_position_index.shape[1]
    cap_slots = max(2, 2 * length_total // devices)
    owner_users = hist_owner[0, :, 0]
    owner_hot = (owner_users[:, None] == jnp.arange(devices, dtype=jnp.int32)[None, :]).astype(
        jnp.int32
    )
    earlier = jnp.cumsum(owner_hot, axis=0) - owner_hot
    rank_in = jnp.sum(owner_hot * earlier, axis=1)
    position = owner_users * cap_slots + rank_in
    request = (
        jnp.full((devices * cap_slots,), count, jnp.int32)
        .at[position]
        .set(history_position_index[0])
    )
    request = request.reshape(devices, cap_slots)
    width = item_embed.shape[1]
    incoming = lax.all_to_all(request, ("grp", "fsdp"), split_axis=0, concat_axis=0, tiled=True)
    found = serve_rows(incoming, item_embed)
    returned = lax.all_to_all(found, ("grp", "fsdp"), split_axis=0, concat_axis=0, tiled=True)
    fetched = jnp.take(returned.reshape(devices * cap_slots, width), position, axis=0)
    hidden = stored(
        jnp.einsum("td,gdc->tgc", fetched, adapter_halves, preferred_element_type=jnp.float32).reshape(
            fetched.shape[0], -1
        )
    )
    user_attention_output, pull = jax.vjp(
        lambda values: user_layer(values, user_gain, query_map), hidden
    )
    (grad_hidden,) = pull(cotangent[0])
    slot_of = (
        position[None, :] == jnp.arange(devices * cap_slots, dtype=jnp.int32)[:, None]
    ).astype(grad_hidden.dtype)
    slot_grads = jnp.dot(slot_of, grad_hidden, preferred_element_type=jnp.float32).astype(
        grad_hidden.dtype
    )
    outgoing = jnp.einsum(
        "tgc,gdc->td",
        slot_grads.reshape(slot_grads.shape[0], groups, -1),
        adapter_halves,
        preferred_element_type=jnp.float32,
    ).astype(jnp.bfloat16)
    arrived = lax.all_to_all(
        outgoing.reshape(devices, cap_slots, DI),
        ("grp", "fsdp"),
        split_axis=0,
        concat_axis=0,
        tiled=True,
    ).astype(jnp.float32)
    terms = arrived.reshape(devices * cap_slots, DI)
    slot_hot = (
        incoming.reshape(-1)[:, None] == jnp.arange(count, dtype=jnp.int32)[None, :]
    ).astype(jnp.float32)
    item_grad = jnp.dot(slot_hot.T, terms, precision=lax.Precision.HIGHEST)
    return (item_embed, user_attention_output[None], item_grad)


def solution(mesh):
    placed = (
        P(("grp", "fsdp"), None, None),
        P("fsdp", None),
        P("fsdp", None),
        P("fsdp", None),
        P(),
        P("fsdp", None),
        P(),
        P("fsdp", None),
        P(("grp", "fsdp"), None, None),
        P(("grp", "fsdp"), None),
        P(("grp", "fsdp"), None, None),
    )
    return jax.shard_map(
        per_device,
        mesh=mesh,
        in_specs=placed,
        out_specs=(
            P(("grp", "fsdp"), None),
            P(("grp", "fsdp"), None, None),
            P(("grp", "fsdp"), None),
        ),
        check_vma=False,
    )
```

```python
import jax
import jax.numpy as jnp
from jax import lax
from jax.experimental import pallas as pl
from jax.experimental.pallas import tpu as pltpu
from jax.sharding import PartitionSpec as P

DI = 2048
IHEADS = 32
IHD = 64
IKV = 4
UHEADS = 32
UHD = 128
ILEN = 256


def stored(values):
    return lax.optimization_barrier(values.astype(jnp.bfloat16))


def rms_scale(values, gain):
    mean_sq = jnp.mean(values * values, axis=-1, keepdims=True)
    return values * lax.rsqrt(mean_sq + 1e-05) * gain


def item_pool(states, key_rows, value_rows, query_rows, item_gain):
    count = states.shape[0]
    group = IHEADS // IKV
    query_heads = query_rows.reshape(count, IKV, group, IHD).astype(jnp.float32)
    key_heads = key_rows.reshape(count, ILEN, IKV, IHD).astype(jnp.float32)
    value_heads = value_rows.reshape(count, ILEN, IKV, IHD).astype(jnp.float32)
    scores = jnp.einsum("igrd,itgd->igrt", query_heads, key_heads) * IHD ** (-0.5)
    weights = stored(jax.nn.softmax(scores, axis=-1)).astype(jnp.float32)
    mixed = jnp.einsum("igrt,itgd->igrd", weights, value_heads).reshape(count, IHEADS * IHD)
    last_row = states[:, ILEN - 1, :].astype(jnp.float32)
    return rms_scale(last_row + mixed, item_gain).astype(jnp.bfloat16)


def user_layer(hidden, user_gain, user_query):
    length_total = hidden.shape[0]
    normed = stored(rms_scale(hidden.astype(jnp.float32), user_gain)).astype(jnp.float32)
    heads = normed.reshape(length_total, UHEADS, UHD)
    query_map = user_query.reshape(UHEADS, UHD, UHD).astype(jnp.float32)
    queries = stored(jnp.einsum("thd,hde->the", heads, query_map)).astype(jnp.float32)
    scores = jnp.einsum("the,she->hts", queries, heads) * UHD ** (-0.5)
    target = jnp.arange(length_total, dtype=jnp.int32)
    causal = target[None, :, None] >= target[None, None, :]
    scores = jnp.where(causal, scores, -1e30)
    weights = stored(jax.nn.softmax(scores, axis=-1)).astype(jnp.float32)
    mixed = jnp.einsum("hts,shd->thd", weights, heads).reshape(length_total, UHEADS * UHD)
    return (hidden.astype(jnp.float32) + mixed).astype(jnp.bfloat16)


def _pack_halves(*refs):
    sources, out = refs[:-1], refs[-1]
    first = lax.axis_index("grp") == 0
    column = 0
    for i, src in enumerate(sources):
        if i == len(sources) - 1:
            rows = src.shape[0] // 2
            width = src.shape[1]
            low, high = src[:rows, :], src[rows:, :]
        else:
            width = src.shape[1] // 2
            low, high = src[:, :width], src[:, width:]
        out[:, column : column + width] = jnp.where(first, low, high)
        column += width


def pack_halves(sources):
    total = sum(w.shape[1] // 2 for w in sources[:-1]) + sources[-1].shape[1]
    return pl.pallas_call(
        _pack_halves,
        out_shape=jax.ShapeDtypeStruct((sources[0].shape[0], total), sources[0].dtype),
    )(*sources)


def serve_rows(requests, lookup_matrix):
    chosen_items = (
        requests[..., None] == jnp.arange(lookup_matrix.shape[0], dtype=jnp.int32)
    ).astype(lookup_matrix.dtype)
    return jnp.einsum(
        "ltj,jy->lty", chosen_items, lookup_matrix, preferred_element_type=jnp.float32
    ).astype(lookup_matrix.dtype)


def per_device(
    item_states,
    w_query,
    w_key,
    w_value,
    item_gain,
    w_adapt,
    user_gain,
    user_query,
    hist_owner,
    history_position_index,
    cotangent,
):
    groups = lax.axis_size("grp")
    shards = lax.axis_size("fsdp")
    devices = groups * shards
    count = item_states.shape[0]
    flat = item_states.reshape(count * ILEN, DI)
    last_row = item_states[:, ILEN - 1, :]
    side = lax.axis_index("grp")

    sources = [w_key, w_value, w_query, w_adapt, user_query]
    widths = [w.shape[1] // 2 for w in sources[:-1]] + [user_query.shape[1]]
    ends = [sum(widths[: i + 1]) for i in range(len(widths))]
    gathered = lax.all_gather(
        pack_halves(sources), ("grp", "fsdp"), axis=0, tiled=True
    ).reshape(groups, DI, ends[-1])
    kv_sum = jnp.einsum(
        "td,gdc->tgc", flat, gathered[:, :, : ends[1]], preferred_element_type=jnp.float32
    )
    key_sum = kv_sum[:, :, : widths[0]].reshape(flat.shape[0], -1)
    summed_value = kv_sum[:, :, widths[0] :].reshape(flat.shape[0], -1)
    query_sum = jnp.einsum(
        "id,gdc->igc", last_row, gathered[:, :, ends[1] : ends[2]], preferred_element_type=jnp.float32
    ).reshape(count, -1)
    adapter_halves = gathered[:, :, ends[2] : ends[3]]
    query_map = (
        gathered[:, :, ends[3] :]
        .reshape(groups, shards, -1, user_query.shape[1])
        .transpose(1, 0, 2, 3)
        .reshape(-1, user_query.shape[1])
    )
    item_embed = item_pool(
        item_states, stored(key_sum), stored(summed_value), stored(query_sum), item_gain
    )
    length_total = history_position_index.shape[1]
    cap_slots = max(2, 2 * length_total // devices)
    owner_users = hist_owner[0, :, 0]
    owner_hot = (owner_users[:, None] == jnp.arange(devices, dtype=jnp.int32)[None, :]).astype(
        jnp.int32
    )
    earlier = jnp.cumsum(owner_hot, axis=0) - owner_hot
    rank_in = jnp.sum(owner_hot * earlier, axis=1)
    position = owner_users * cap_slots + rank_in
    request = (
        jnp.full((devices * cap_slots,), count, jnp.int32)
        .at[position]
        .set(history_position_index[0])
    )
    request = request.reshape(devices, cap_slots)
    width = item_embed.shape[1]
    incoming = lax.all_to_all(request, ("grp", "fsdp"), split_axis=0, concat_axis=0, tiled=True)
    found = jnp.take(
        jnp.concatenate([item_embed, jnp.zeros((1, item_embed.shape[1]), item_embed.dtype)], axis=0),
        jnp.clip(incoming, 0, count),
        axis=0,
    )
    returned = lax.all_to_all(found, ("grp", "fsdp"), split_axis=0, concat_axis=0, tiled=True)
    fetched = jnp.take(returned.reshape(devices * cap_slots, width), position, axis=0)
    hidden = stored(
        jnp.einsum("td,gdc->tgc", fetched, adapter_halves, preferred_element_type=jnp.float32).reshape(
            fetched.shape[0], -1
        )
    )
    user_attention_output, pull = jax.vjp(
        lambda values: user_layer(values, user_gain, query_map), hidden
    )
    (grad_hidden,) = pull(cotangent[0])
    slot_of = (
        position[None, :] == jnp.arange(devices * cap_slots, dtype=jnp.int32)[:, None]
    ).astype(grad_hidden.dtype)
    slot_grads = jnp.dot(slot_of, grad_hidden, preferred_element_type=jnp.float32).astype(
        grad_hidden.dtype
    )
    outgoing = jnp.einsum(
        "tgc,gdc->td",
        slot_grads.reshape(slot_grads.shape[0], groups, -1),
        adapter_halves,
        preferred_element_type=jnp.float32,
    ).astype(jnp.bfloat16)
    arrived = lax.all_to_all(
        outgoing.reshape(devices, cap_slots, DI),
        ("grp", "fsdp"),
        split_axis=0,
        concat_axis=0,
        tiled=True,
    ).astype(jnp.float32)
    terms = arrived.reshape(devices * cap_slots, DI)
    slot_hot = (
        incoming.reshape(-1)[:, None] == jnp.arange(count, dtype=jnp.int32)[None, :]
    ).astype(jnp.float32)
    item_grad = jnp.dot(slot_hot.T, terms, precision=lax.Precision.HIGHEST)
    return (item_embed, user_attention_output[None], item_grad)


def solution(mesh):
    placed = (
        P(("grp", "fsdp"), None, None),
        P("fsdp", None),
        P("fsdp", None),
        P("fsdp", None),
        P(),
        P("fsdp", None),
        P(),
        P("fsdp", None),
        P(("grp", "fsdp"), None, None),
        P(("grp", "fsdp"), None),
        P(("grp", "fsdp"), None, None),
    )
    return jax.shard_map(
        per_device,
        mesh=mesh,
        in_specs=placed,
        out_specs=(
            P(("grp", "fsdp"), None),
            P(("grp", "fsdp"), None, None),
            P(("grp", "fsdp"), None),
        ),
        check_vma=False,
    )
```

```python
import jax
import jax.numpy as jnp
from jax import lax
from jax.experimental import pallas as pl
from jax.experimental.pallas import tpu as pltpu
from jax.sharding import PartitionSpec as P

DI = 2048
IHEADS = 32
IHD = 64
IKV = 4
UHEADS = 32
UHD = 128
ILEN = 256


def stored(values):
    return lax.optimization_barrier(values.astype(jnp.bfloat16))


def rms_scale(values, gain):
    mean_sq = jnp.mean(values * values, axis=-1, keepdims=True)
    return values * lax.rsqrt(mean_sq + 1e-05) * gain


def item_pool(states, key_rows, value_rows, query_rows, item_gain):
    count = states.shape[0]
    group = IHEADS // IKV
    query_heads = query_rows.reshape(count, IKV, group, IHD).astype(jnp.float32)
    key_heads = key_rows.reshape(count, ILEN, IKV, IHD).astype(jnp.float32)
    value_heads = value_rows.reshape(count, ILEN, IKV, IHD).astype(jnp.float32)
    scores = jnp.einsum("igrd,itgd->igrt", query_heads, key_heads) * IHD ** (-0.5)
    weights = stored(jax.nn.softmax(scores, axis=-1)).astype(jnp.float32)
    mixed = jnp.einsum("igrt,itgd->igrd", weights, value_heads).reshape(count, IHEADS * IHD)
    last_row = states[:, ILEN - 1, :].astype(jnp.float32)
    return rms_scale(last_row + mixed, item_gain).astype(jnp.bfloat16)


def user_layer(hidden, user_gain, user_query):
    length_total = hidden.shape[0]
    normed = stored(rms_scale(hidden.astype(jnp.float32), user_gain)).astype(jnp.float32)
    heads = normed.reshape(length_total, UHEADS, UHD)
    query_map = user_query.reshape(UHEADS, UHD, UHD).astype(jnp.float32)
    queries = stored(jnp.einsum("thd,hde->the", heads, query_map)).astype(jnp.float32)
    scores = jnp.einsum("the,she->hts", queries, heads) * UHD ** (-0.5)
    target = jnp.arange(length_total, dtype=jnp.int32)
    causal = target[None, :, None] >= target[None, None, :]
    scores = jnp.where(causal, scores, -1e30)
    weights = stored(jax.nn.softmax(scores, axis=-1)).astype(jnp.float32)
    mixed = jnp.einsum("hts,shd->thd", weights, heads).reshape(length_total, UHEADS * UHD)
    return (hidden.astype(jnp.float32) + mixed).astype(jnp.bfloat16)


def _pack_halves(*refs):
    sources, out = refs[:-1], refs[-1]
    first = lax.axis_index("grp") == 0
    column = 0
    for i, src in enumerate(sources):
        if i == len(sources) - 1:
            rows = src.shape[0] // 2
            width = src.shape[1]
            low, high = src[:rows, :], src[rows:, :]
        else:
            width = src.shape[1] // 2
            low, high = src[:, :width], src[:, width:]
        out[:, column : column + width] = jnp.where(first, low, high)
        column += width


def pack_halves(sources):
    total = sum(w.shape[1] // 2 for w in sources[:-1]) + sources[-1].shape[1]
    return pl.pallas_call(
        _pack_halves,
        out_shape=jax.ShapeDtypeStruct((sources[0].shape[0], total), sources[0].dtype),
    )(*sources)


def serve_rows(requests, lookup_matrix):
    chosen_items = (
        requests[..., None] == jnp.arange(lookup_matrix.shape[0], dtype=jnp.int32)
    ).astype(lookup_matrix.dtype)
    return jnp.einsum(
        "ltj,jy->lty", chosen_items, lookup_matrix, preferred_element_type=jnp.float32
    ).astype(lookup_matrix.dtype)


def per_device(
    item_states,
    w_query,
    w_key,
    w_value,
    item_gain,
    w_adapt,
    user_gain,
    user_query,
    hist_owner,
    history_position_index,
    cotangent,
):
    groups = lax.axis_size("grp")
    shards = lax.axis_size("fsdp")
    devices = groups * shards
    count = item_states.shape[0]
    flat = item_states.reshape(count * ILEN, DI)
    last_row = item_states[:, ILEN - 1, :]
    side = lax.axis_index("grp")

    sources = [w_key, w_value, w_query, w_adapt, user_query]
    widths = [w.shape[1] // 2 for w in sources[:-1]] + [user_query.shape[1]]
    ends = [sum(widths[: i + 1]) for i in range(len(widths))]
    gathered = lax.all_gather(
        pack_halves(sources), ("grp", "fsdp"), axis=0, tiled=True
    ).reshape(groups, DI, ends[-1])
    kv_sum = jnp.einsum(
        "td,gdc->tgc", flat, gathered[:, :, : ends[1]], preferred_element_type=jnp.float32
    )
    key_sum = kv_sum[:, :, : widths[0]].reshape(flat.shape[0], -1)
    summed_value = kv_sum[:, :, widths[0] :].reshape(flat.shape[0], -1)
    query_sum = jnp.einsum(
        "id,gdc->igc", last_row, gathered[:, :, ends[1] : ends[2]], preferred_element_type=jnp.float32
    ).reshape(count, -1)
    adapter_halves = gathered[:, :, ends[2] : ends[3]]
    query_map = (
        gathered[:, :, ends[3] :]
        .reshape(groups, shards, -1, user_query.shape[1])
        .transpose(1, 0, 2, 3)
        .reshape(-1, user_query.shape[1])
    )
    item_embed = item_pool(
        item_states, stored(key_sum), stored(summed_value), stored(query_sum), item_gain
    )
    length_total = history_position_index.shape[1]
    cap_slots = max(2, 2 * length_total // devices)
    owner_users = hist_owner[0, :, 0]
    owner_hot = (owner_users[:, None] == jnp.arange(devices, dtype=jnp.int32)[None, :]).astype(
        jnp.int32
    )
    earlier = jnp.cumsum(owner_hot, axis=0) - owner_hot
    rank_in = jnp.sum(owner_hot * earlier, axis=1)
    position = owner_users * cap_slots + rank_in
    request = (
        jnp.full((devices * cap_slots,), count, jnp.int32)
        .at[position]
        .set(history_position_index[0])
    )
    request = request.reshape(devices, cap_slots)
    width = item_embed.shape[1]
    incoming = lax.all_to_all(request, ("grp", "fsdp"), split_axis=0, concat_axis=0, tiled=True)
    found = jnp.take(
        jnp.concatenate([item_embed, jnp.zeros((1, item_embed.shape[1]), item_embed.dtype)], axis=0),
        jnp.clip(incoming, 0, count),
        axis=0,
        mode="clip",
    )
    returned = lax.all_to_all(found, ("grp", "fsdp"), split_axis=0, concat_axis=0, tiled=True)
    fetched = jnp.take(returned.reshape(devices * cap_slots, width), position, axis=0)
    hidden = stored(
        jnp.einsum("td,gdc->tgc", fetched, adapter_halves, preferred_element_type=jnp.float32).reshape(
            fetched.shape[0], -1
        )
    )
    user_attention_output, pull = jax.vjp(
        lambda values: user_layer(values, user_gain, query_map), hidden
    )
    (grad_hidden,) = pull(cotangent[0])
    slot_of = (
        position[None, :] == jnp.arange(devices * cap_slots, dtype=jnp.int32)[:, None]
    ).astype(grad_hidden.dtype)
    slot_grads = jnp.dot(slot_of, grad_hidden, preferred_element_type=jnp.float32).astype(
        grad_hidden.dtype
    )
    outgoing = jnp.einsum(
        "tgc,gdc->td",
        slot_grads.reshape(slot_grads.shape[0], groups, -1),
        adapter_halves,
        preferred_element_type=jnp.float32,
    ).astype(jnp.bfloat16)
    arrived = lax.all_to_all(
        outgoing.reshape(devices, cap_slots, DI),
        ("grp", "fsdp"),
        split_axis=0,
        concat_axis=0,
        tiled=True,
    ).astype(jnp.float32)
    terms = arrived.reshape(devices * cap_slots, DI)
    slot_hot = (
        incoming.reshape(-1)[:, None] == jnp.arange(count, dtype=jnp.int32)[None, :]
    ).astype(jnp.float32)
    item_grad = jnp.dot(slot_hot.T, terms, precision=lax.Precision.HIGHEST)
    return (item_embed, user_attention_output[None], item_grad)


def solution(mesh):
    placed = (
        P(("grp", "fsdp"), None, None),
        P("fsdp", None),
        P("fsdp", None),
        P("fsdp", None),
        P(),
        P("fsdp", None),
        P(),
        P("fsdp", None),
        P(("grp", "fsdp"), None, None),
        P(("grp", "fsdp"), None),
        P(("grp", "fsdp"), None, None),
    )
    return jax.shard_map(
        per_device,
        mesh=mesh,
        in_specs=placed,
        out_specs=(
            P(("grp", "fsdp"), None),
            P(("grp", "fsdp"), None, None),
            P(("grp", "fsdp"), None),
        ),
        check_vma=False,
    )
```

```python
import jax
import jax.numpy as jnp
from jax import lax
from jax.experimental import pallas as pl
from jax.experimental.pallas import tpu as pltpu
from jax.sharding import PartitionSpec as P

DI = 2048
IHEADS = 32
IHD = 64
IKV = 4
UHEADS = 32
UHD = 128
ILEN = 256


def stored(values):
    return lax.optimization_barrier(values.astype(jnp.bfloat16))


def rms_scale(values, gain):
    mean_sq = jnp.mean(values * values, axis=-1, keepdims=True)
    return values * lax.rsqrt(mean_sq + 1e-05) * gain


def item_pool(states, key_rows, value_rows, query_rows, item_gain):
    count = states.shape[0]
    group = IHEADS // IKV
    query_heads = query_rows.reshape(count, IKV, group, IHD).astype(jnp.float32)
    key_heads = key_rows.reshape(count, ILEN, IKV, IHD).astype(jnp.float32)
    value_heads = value_rows.reshape(count, ILEN, IKV, IHD).astype(jnp.float32)
    scores = jnp.einsum("igrd,itgd->igrt", query_heads, key_heads) * IHD ** (-0.5)
    weights = stored(jax.nn.softmax(scores, axis=-1)).astype(jnp.float32)
    mixed = jnp.einsum("igrt,itgd->igrd", weights, value_heads).reshape(count, IHEADS * IHD)
    last_row = states[:, ILEN - 1, :].astype(jnp.float32)
    return rms_scale(last_row + mixed, item_gain).astype(jnp.bfloat16)


def user_layer(hidden, user_gain, user_query):
    length_total = hidden.shape[0]
    normed = stored(rms_scale(hidden.astype(jnp.float32), user_gain)).astype(jnp.float32)
    heads = normed.reshape(length_total, UHEADS, UHD)
    query_map = user_query.reshape(UHEADS, UHD, UHD).astype(jnp.float32)
    queries = stored(jnp.einsum("thd,hde->the", heads, query_map)).astype(jnp.float32)
    scores = jnp.einsum("the,she->hts", queries, heads) * UHD ** (-0.5)
    target = jnp.arange(length_total, dtype=jnp.int32)
    causal = target[None, :, None] >= target[None, None, :]
    scores = jnp.where(causal, scores, -1e30)
    weights = stored(jax.nn.softmax(scores, axis=-1)).astype(jnp.float32)
    mixed = jnp.einsum("hts,shd->thd", weights, heads).reshape(length_total, UHEADS * UHD)
    return (hidden.astype(jnp.float32) + mixed).astype(jnp.bfloat16)


def _pack_halves(*refs):
    sources, out = refs[:-1], refs[-1]
    first = lax.axis_index("grp") == 0
    column = 0
    for i, src in enumerate(sources):
        if i == len(sources) - 1:
            rows = src.shape[0] // 2
            width = src.shape[1]
            low, high = src[:rows, :], src[rows:, :]
        else:
            width = src.shape[1] // 2
            low, high = src[:, :width], src[:, width:]
        out[:, column : column + width] = jnp.where(first, low, high)
        column += width


def pack_halves(sources):
    total = sum(w.shape[1] // 2 for w in sources[:-1]) + sources[-1].shape[1]
    return pl.pallas_call(
        _pack_halves,
        out_shape=jax.ShapeDtypeStruct((sources[0].shape[0], total), sources[0].dtype),
    )(*sources)


def ring_gather(block, strides, shards):
    for stride in strides:
        base = [f for f in range(shards) if (f // stride) % 4 == 0]
        up = [(f + k * stride, f + ((k + 1) % 4) * stride) for f in base for k in range(4)]
        down = [(b, a) for a, b in up]
        from_below = lax.ppermute(block, "fsdp", up)
        from_above = lax.ppermute(block, "fsdp", down)
        from_two_up = lax.ppermute(from_above, "fsdp", down)
        relative = jnp.stack([block, from_above, from_two_up, from_below])
        place = (lax.axis_index("fsdp") // stride) % 4
        block = jnp.roll(relative, place, axis=0)
    return block


def serve_rows(requests, lookup_matrix):
    chosen_items = (
        requests[..., None] == jnp.arange(lookup_matrix.shape[0], dtype=jnp.int32)
    ).astype(lookup_matrix.dtype)
    return jnp.einsum(
        "ltj,jy->lty", chosen_items, lookup_matrix, preferred_element_type=jnp.float32
    ).astype(lookup_matrix.dtype)


def per_device(
    item_states,
    w_query,
    w_key,
    w_value,
    item_gain,
    w_adapt,
    user_gain,
    user_query,
    hist_owner,
    history_position_index,
    cotangent,
):
    groups = lax.axis_size("grp")
    shards = lax.axis_size("fsdp")
    devices = groups * shards
    count = item_states.shape[0]
    flat = item_states.reshape(count * ILEN, DI)
    last_row = item_states[:, ILEN - 1, :]
    side = lax.axis_index("grp")

    sources = [w_key, w_value, w_adapt, user_query]
    widths = [w.shape[1] // 2 for w in sources[:-1]] + [user_query.shape[1]]
    ends = [sum(widths[: i + 1]) for i in range(len(widths))]
    gathered = lax.all_gather(
        pack_halves(sources), ("grp", "fsdp"), axis=0, tiled=True
    ).reshape(groups, DI, ends[-1])
    query_half = w_query.shape[1] // groups
    own_query = lax.dynamic_slice_in_dim(w_query, side * query_half, query_half, axis=1)
    own_query = ring_gather(own_query, (1, 4, 16), shards).reshape(DI, query_half)
    other_query = lax.ppermute(own_query, "grp", [(0, 1), (1, 0)])
    query_own = jnp.dot(last_row, own_query, preferred_element_type=jnp.float32)
    query_other = jnp.dot(last_row, other_query, preferred_element_type=jnp.float32)
    query_sum = jnp.where(
        side == 0,
        jnp.concatenate([query_own, query_other], axis=1),
        jnp.concatenate([query_other, query_own], axis=1),
    )
    kv_sum = jnp.einsum(
        "td,gdc->tgc", flat, gathered[:, :, : ends[1]], preferred_element_type=jnp.float32
    )
    key_sum = kv_sum[:, :, : widths[0]].reshape(flat.shape[0], -1)
    summed_value = kv_sum[:, :, widths[0] :].reshape(flat.shape[0], -1)
    adapter_halves = gathered[:, :, ends[1] : ends[2]]
    query_map = (
        gathered[:, :, ends[2] :]
        .reshape(groups, shards, -1, user_query.shape[1])
        .transpose(1, 0, 2, 3)
        .reshape(-1, user_query.shape[1])
    )
    item_embed = item_pool(
        item_states, stored(key_sum), stored(summed_value), stored(query_sum), item_gain
    )
    length_total = history_position_index.shape[1]
    cap_slots = max(2, 2 * length_total // devices)
    owner_users = hist_owner[0, :, 0]
    owner_hot = (owner_users[:, None] == jnp.arange(devices, dtype=jnp.int32)[None, :]).astype(
        jnp.int32
    )
    earlier = jnp.cumsum(owner_hot, axis=0) - owner_hot
    rank_in = jnp.sum(owner_hot * earlier, axis=1)
    position = owner_users * cap_slots + rank_in
    request = (
        jnp.full((devices * cap_slots,), count, jnp.int32)
        .at[position]
        .set(history_position_index[0])
    )
    request = request.reshape(devices, cap_slots)
    width = item_embed.shape[1]
    incoming = lax.all_to_all(request, ("grp", "fsdp"), split_axis=0, concat_axis=0, tiled=True)
    found = serve_rows(incoming, item_embed)
    returned = lax.all_to_all(found, ("grp", "fsdp"), split_axis=0, concat_axis=0, tiled=True)
    fetched = jnp.take(returned.reshape(devices * cap_slots, width), position, axis=0)
    hidden = stored(
        jnp.einsum("td,gdc->tgc", fetched, adapter_halves, preferred_element_type=jnp.float32).reshape(
            fetched.shape[0], -1
        )
    )
    user_attention_output, pull = jax.vjp(
        lambda values: user_layer(values, user_gain, query_map), hidden
    )
    (grad_hidden,) = pull(cotangent[0])
    slot_of = (
        position[None, :] == jnp.arange(devices * cap_slots, dtype=jnp.int32)[:, None]
    ).astype(grad_hidden.dtype)
    slot_grads = jnp.dot(slot_of, grad_hidden, preferred_element_type=jnp.float32).astype(
        grad_hidden.dtype
    )
    outgoing = jnp.einsum(
        "tgc,gdc->td",
        slot_grads.reshape(slot_grads.shape[0], groups, -1),
        adapter_halves,
        preferred_element_type=jnp.float32,
    ).astype(jnp.bfloat16)
    arrived = lax.all_to_all(
        outgoing.reshape(devices, cap_slots, DI),
        ("grp", "fsdp"),
        split_axis=0,
        concat_axis=0,
        tiled=True,
    ).astype(jnp.float32)
    terms = arrived.reshape(devices * cap_slots, DI)
    slot_hot = (
        incoming.reshape(-1)[:, None] == jnp.arange(count, dtype=jnp.int32)[None, :]
    ).astype(jnp.float32)
    item_grad = jnp.dot(slot_hot.T, terms, precision=lax.Precision.HIGHEST)
    return (item_embed, user_attention_output[None], item_grad)


def solution(mesh):
    placed = (
        P(("grp", "fsdp"), None, None),
        P("fsdp", None),
        P("fsdp", None),
        P("fsdp", None),
        P(),
        P("fsdp", None),
        P(),
        P("fsdp", None),
        P(("grp", "fsdp"), None, None),
        P(("grp", "fsdp"), None),
        P(("grp", "fsdp"), None, None),
    )
    return jax.shard_map(
        per_device,
        mesh=mesh,
        in_specs=placed,
        out_specs=(
            P(("grp", "fsdp"), None),
            P(("grp", "fsdp"), None, None),
            P(("grp", "fsdp"), None),
        ),
        check_vma=False,
    )
```

```python
import jax
import jax.numpy as jnp
from jax import lax
from jax.experimental import pallas as pl
from jax.experimental.pallas import tpu as pltpu
from jax.sharding import PartitionSpec as P

DI = 2048
IHEADS = 32
IHD = 64
IKV = 4
UHEADS = 32
UHD = 128
ILEN = 256


def stored(values):
    return lax.optimization_barrier(values.astype(jnp.bfloat16))


def rms_scale(values, gain):
    mean_sq = jnp.mean(values * values, axis=-1, keepdims=True)
    return values * lax.rsqrt(mean_sq + 1e-05) * gain


def item_pool(states, key_rows, value_rows, query_rows, item_gain):
    count = states.shape[0]
    group = IHEADS // IKV
    query_heads = query_rows.reshape(count, IKV, group, IHD).astype(jnp.float32)
    key_heads = key_rows.reshape(count, ILEN, IKV, IHD).astype(jnp.float32)
    value_heads = value_rows.reshape(count, ILEN, IKV, IHD).astype(jnp.float32)
    scores = jnp.einsum("igrd,itgd->igrt", query_heads, key_heads) * IHD ** (-0.5)
    weights = stored(jax.nn.softmax(scores, axis=-1)).astype(jnp.float32)
    mixed = jnp.einsum("igrt,itgd->igrd", weights, value_heads).reshape(count, IHEADS * IHD)
    last_row = states[:, ILEN - 1, :].astype(jnp.float32)
    return rms_scale(last_row + mixed, item_gain).astype(jnp.bfloat16)


def user_layer(hidden, user_gain, user_query):
    length_total = hidden.shape[0]
    normed = stored(rms_scale(hidden.astype(jnp.float32), user_gain)).astype(jnp.float32)
    heads = normed.reshape(length_total, UHEADS, UHD)
    query_map = user_query.reshape(UHEADS, UHD, UHD).astype(jnp.float32)
    queries = stored(jnp.einsum("thd,hde->the", heads, query_map)).astype(jnp.float32)
    scores = jnp.einsum("the,she->hts", queries, heads) * UHD ** (-0.5)
    target = jnp.arange(length_total, dtype=jnp.int32)
    causal = target[None, :, None] >= target[None, None, :]
    scores = jnp.where(causal, scores, -1e30)
    weights = stored(jax.nn.softmax(scores, axis=-1)).astype(jnp.float32)
    mixed = jnp.einsum("hts,shd->thd", weights, heads).reshape(length_total, UHEADS * UHD)
    return (hidden.astype(jnp.float32) + mixed).astype(jnp.bfloat16)


def _pack_halves(*refs):
    sources, out = refs[:-1], refs[-1]
    first = lax.axis_index("grp") == 0
    column = 0
    for i, src in enumerate(sources):
        if i == len(sources) - 1:
            rows = src.shape[0] // 2
            width = src.shape[1]
            low, high = src[:rows, :], src[rows:, :]
        else:
            width = src.shape[1] // 2
            low, high = src[:, :width], src[:, width:]
        out[:, column : column + width] = jnp.where(first, low, high)
        column += width


def pack_halves(sources):
    total = sum(w.shape[1] // 2 for w in sources[:-1]) + sources[-1].shape[1]
    return pl.pallas_call(
        _pack_halves,
        out_shape=jax.ShapeDtypeStruct((sources[0].shape[0], total), sources[0].dtype),
    )(*sources)


def serve_rows(requests, lookup_matrix):
    chosen_items = (
        requests[..., None] == jnp.arange(lookup_matrix.shape[0], dtype=jnp.int32)
    ).astype(lookup_matrix.dtype)
    return jnp.einsum(
        "ltj,jy->lty", chosen_items, lookup_matrix, preferred_element_type=jnp.float32
    ).astype(lookup_matrix.dtype)


def per_device(
    item_states,
    w_query,
    w_key,
    w_value,
    item_gain,
    w_adapt,
    user_gain,
    user_query,
    hist_owner,
    history_position_index,
    cotangent,
):
    groups = lax.axis_size("grp")
    shards = lax.axis_size("fsdp")
    devices = groups * shards
    count = item_states.shape[0]
    flat = item_states.reshape(count * ILEN, DI)
    last_row = item_states[:, ILEN - 1, :]
    side = lax.axis_index("grp")

    sources = [w_key, w_value, w_query, w_adapt, user_query]
    widths = [w.shape[1] // 2 for w in sources[:-1]] + [user_query.shape[1]]
    ends = [sum(widths[: i + 1]) for i in range(len(widths))]
    gathered = lax.all_gather(
        pack_halves(sources), ("grp", "fsdp"), axis=0, tiled=True
    ).reshape(groups, DI, ends[-1])
    kv_sum = jnp.einsum(
        "td,gdc->tgc", flat, gathered[:, :, : ends[1]], preferred_element_type=jnp.float32
    )
    key_sum = kv_sum[:, :, : widths[0]].reshape(flat.shape[0], -1)
    summed_value = kv_sum[:, :, widths[0] :].reshape(flat.shape[0], -1)
    query_sum = jnp.einsum(
        "id,gdc->igc", last_row, gathered[:, :, ends[1] : ends[2]], preferred_element_type=jnp.float32
    ).reshape(count, -1)
    adapter_halves = gathered[:, :, ends[2] : ends[3]]
    query_map = (
        gathered[:, :, ends[3] :]
        .reshape(groups, shards, -1, user_query.shape[1])
        .transpose(1, 0, 2, 3)
        .reshape(-1, user_query.shape[1])
    )
    item_embed = item_pool(
        item_states, stored(key_sum), stored(summed_value), stored(query_sum), item_gain
    )
    length_total = history_position_index.shape[1]
    cap_slots = max(2, 2 * length_total // devices)
    owner_users = hist_owner[0, :, 0]
    owner_hot = (owner_users[:, None] == jnp.arange(devices, dtype=jnp.int32)[None, :]).astype(
        jnp.int32
    )
    earlier = jnp.cumsum(owner_hot, axis=0) - owner_hot
    rank_in = jnp.sum(owner_hot * earlier, axis=1)
    position = owner_users * cap_slots + rank_in
    request = (
        jnp.full((devices * cap_slots,), count, jnp.int32)
        .at[position]
        .set(history_position_index[0])
    )
    request = request.reshape(devices, cap_slots)
    width = item_embed.shape[1]
    incoming = lax.all_to_all(request, ("grp", "fsdp"), split_axis=0, concat_axis=0, tiled=True)
    found = serve_rows(incoming, item_embed)
    returned = lax.all_to_all(found, ("grp", "fsdp"), split_axis=0, concat_axis=0, tiled=True)
    fetched = jnp.take(returned.reshape(devices * cap_slots, width), position, axis=0)
    hidden = stored(
        jnp.einsum("td,gdc->tgc", fetched, adapter_halves, preferred_element_type=jnp.float32).reshape(
            fetched.shape[0], -1
        )
    )
    user_attention_output, pull = jax.vjp(
        lambda values: user_layer(values, user_gain, query_map), hidden
    )
    (grad_hidden,) = pull(cotangent[0])
    grad_rows = jnp.einsum(
        "tgc,gdc->td",
        grad_hidden.reshape(grad_hidden.shape[0], groups, -1),
        adapter_halves,
        preferred_element_type=jnp.float32,
    ).astype(jnp.bfloat16)
    slot_of = (
        position[None, :] == jnp.arange(devices * cap_slots, dtype=jnp.int32)[:, None]
    ).astype(grad_rows.dtype)
    outgoing = jnp.dot(slot_of, grad_rows, preferred_element_type=jnp.float32).astype(
        grad_rows.dtype
    )
    arrived = lax.all_to_all(
        outgoing.reshape(devices, cap_slots, DI),
        ("grp", "fsdp"),
        split_axis=0,
        concat_axis=0,
        tiled=True,
    ).astype(jnp.float32)
    terms = arrived.reshape(devices * cap_slots, DI)
    slot_hot = (
        incoming.reshape(-1)[:, None] == jnp.arange(count, dtype=jnp.int32)[None, :]
    ).astype(jnp.float32)
    item_grad = jnp.dot(slot_hot.T, terms, precision=lax.Precision.HIGHEST)
    return (item_embed, user_attention_output[None], item_grad)


def solution(mesh):
    placed = (
        P(("grp", "fsdp"), None, None),
        P("fsdp", None),
        P("fsdp", None),
        P("fsdp", None),
        P(),
        P("fsdp", None),
        P(),
        P("fsdp", None),
        P(("grp", "fsdp"), None, None),
        P(("grp", "fsdp"), None),
        P(("grp", "fsdp"), None, None),
    )
    return jax.shard_map(
        per_device,
        mesh=mesh,
        in_specs=placed,
        out_specs=(
            P(("grp", "fsdp"), None),
            P(("grp", "fsdp"), None, None),
            P(("grp", "fsdp"), None),
        ),
        check_vma=False,
    )
```

```python
import jax
import jax.numpy as jnp
from jax import lax
from jax.experimental import pallas as pl
from jax.experimental.pallas import tpu as pltpu
from jax.sharding import PartitionSpec as P

DI = 2048
IHEADS = 32
IHD = 64
IKV = 4
UHEADS = 32
UHD = 128
ILEN = 256


def stored(values):
    return lax.optimization_barrier(values.astype(jnp.bfloat16))


def rms_scale(values, gain):
    mean_sq = jnp.mean(values * values, axis=-1, keepdims=True)
    return values * lax.rsqrt(mean_sq + 1e-05) * gain


def item_pool(states, key_rows, value_rows, query_rows, item_gain):
    count = states.shape[0]
    group = IHEADS // IKV
    query_heads = query_rows.reshape(count, IKV, group, IHD).astype(jnp.float32)
    key_heads = key_rows.reshape(count, ILEN, IKV, IHD).astype(jnp.float32)
    value_heads = value_rows.reshape(count, ILEN, IKV, IHD).astype(jnp.float32)
    scores = jnp.einsum("igrd,itgd->igrt", query_heads, key_heads) * IHD ** (-0.5)
    weights = stored(jax.nn.softmax(scores, axis=-1)).astype(jnp.float32)
    mixed = jnp.einsum("igrt,itgd->igrd", weights, value_heads).reshape(count, IHEADS * IHD)
    last_row = states[:, ILEN - 1, :].astype(jnp.float32)
    return rms_scale(last_row + mixed, item_gain).astype(jnp.bfloat16)


def user_layer(hidden, user_gain, user_query):
    length_total = hidden.shape[0]
    normed = stored(rms_scale(hidden.astype(jnp.float32), user_gain)).astype(jnp.float32)
    heads = normed.reshape(length_total, UHEADS, UHD)
    query_map = user_query.reshape(UHEADS, UHD, UHD).astype(jnp.float32)
    queries = stored(jnp.einsum("thd,hde->the", heads, query_map)).astype(jnp.float32)
    scores = jnp.einsum("the,she->hts", queries, heads) * UHD ** (-0.5)
    target = jnp.arange(length_total, dtype=jnp.int32)
    causal = target[None, :, None] >= target[None, None, :]
    scores = jnp.where(causal, scores, -1e30)
    weights = stored(jax.nn.softmax(scores, axis=-1)).astype(jnp.float32)
    mixed = jnp.einsum("hts,shd->thd", weights, heads).reshape(length_total, UHEADS * UHD)
    return (hidden.astype(jnp.float32) + mixed).astype(jnp.bfloat16)


def _pack_halves(*refs):
    sources, out = refs[:-1], refs[-1]
    first = lax.axis_index("grp") == 0
    column = 0
    for i, src in enumerate(sources):
        if i == len(sources) - 1:
            rows = src.shape[0] // 2
            width = src.shape[1]
            low, high = src[:rows, :], src[rows:, :]
        else:
            width = src.shape[1] // 2
            low, high = src[:, :width], src[:, width:]
        out[:, column : column + width] = jnp.where(first, low, high)
        column += width


def pack_halves(sources):
    total = sum(w.shape[1] // 2 for w in sources[:-1]) + sources[-1].shape[1]
    return pl.pallas_call(
        _pack_halves,
        out_shape=jax.ShapeDtypeStruct((sources[0].shape[0], total), sources[0].dtype),
    )(*sources)


def serve_rows(requests, lookup_matrix):
    chosen_items = (
        requests[..., None] == jnp.arange(lookup_matrix.shape[0], dtype=jnp.int32)
    ).astype(lookup_matrix.dtype)
    return jnp.einsum(
        "ltj,jy->lty", chosen_items, lookup_matrix, preferred_element_type=jnp.float32
    ).astype(lookup_matrix.dtype)


def per_device(
    item_states,
    w_query,
    w_key,
    w_value,
    item_gain,
    w_adapt,
    user_gain,
    user_query,
    hist_owner,
    history_position_index,
    cotangent,
):
    groups = lax.axis_size("grp")
    shards = lax.axis_size("fsdp")
    devices = groups * shards
    count = item_states.shape[0]
    flat = item_states.reshape(count * ILEN, DI)
    last_row = item_states[:, ILEN - 1, :]
    side = lax.axis_index("grp")

    sources = [w_key, w_value, w_query, w_adapt, user_query]
    widths = [w.shape[1] // 2 for w in sources[:-1]] + [user_query.shape[1]]
    ends = [sum(widths[: i + 1]) for i in range(len(widths))]
    gathered = lax.all_gather(
        pack_halves(sources), ("grp", "fsdp"), axis=0, tiled=True
    ).reshape(groups, DI, ends[-1])
    kv_sum = jnp.einsum(
        "td,gdc->tgc", flat, gathered[:, :, : ends[1]], preferred_element_type=jnp.float32
    )
    key_sum = kv_sum[:, :, : widths[0]].reshape(flat.shape[0], -1)
    summed_value = kv_sum[:, :, widths[0] :].reshape(flat.shape[0], -1)
    query_sum = jnp.einsum(
        "id,gdc->igc", last_row, gathered[:, :, ends[1] : ends[2]], preferred_element_type=jnp.float32
    ).reshape(count, -1)
    adapter_halves = gathered[:, :, ends[2] : ends[3]]
    query_map = (
        gathered[:, :, ends[3] :]
        .reshape(groups, shards, -1, user_query.shape[1])
        .transpose(1, 0, 2, 3)
        .reshape(-1, user_query.shape[1])
    )
    item_embed = item_pool(
        item_states, stored(key_sum), stored(summed_value), stored(query_sum), item_gain
    )
    length_total = history_position_index.shape[1]
    cap_slots = max(2, 2 * length_total // devices)
    owner_users = hist_owner[0, :, 0]
    owner_hot = (owner_users[:, None] == jnp.arange(devices, dtype=jnp.int32)[None, :]).astype(
        jnp.int32
    )
    earlier = jnp.cumsum(owner_hot, axis=0) - owner_hot
    rank_in = jnp.sum(owner_hot * earlier, axis=1)
    position = owner_users * cap_slots + rank_in
    request = (
        jnp.full((devices * cap_slots,), count, jnp.int32)
        .at[position]
        .set(history_position_index[0])
    )
    request = request.reshape(devices, cap_slots)
    width = item_embed.shape[1]
    incoming = lax.all_to_all(request, ("grp", "fsdp"), split_axis=0, concat_axis=0, tiled=True)
    found = jnp.swapaxes(serve_rows(incoming, item_embed), 0, 1)
    returned = lax.all_to_all(found, ("grp", "fsdp"), split_axis=1, concat_axis=1, tiled=True)
    fetched = jnp.take(
        returned.reshape(devices * cap_slots, width), rank_in * devices + owner_users, axis=0
    )
    hidden = stored(
        jnp.einsum("td,gdc->tgc", fetched, adapter_halves, preferred_element_type=jnp.float32).reshape(
            fetched.shape[0], -1
        )
    )
    user_attention_output, pull = jax.vjp(
        lambda values: user_layer(values, user_gain, query_map), hidden
    )
    (grad_hidden,) = pull(cotangent[0])
    grad_rows = jnp.einsum(
        "tgc,gdc->td",
        grad_hidden.reshape(grad_hidden.shape[0], groups, -1),
        adapter_halves,
        preferred_element_type=jnp.float32,
    ).astype(jnp.bfloat16)
    slot_of = (
        (rank_in * devices + owner_users)[None, :]
        == jnp.arange(devices * cap_slots, dtype=jnp.int32)[:, None]
    ).astype(grad_rows.dtype)
    outgoing = jnp.dot(slot_of, grad_rows, preferred_element_type=jnp.float32).astype(
        grad_rows.dtype
    )
    arrived = lax.all_to_all(
        outgoing.reshape(cap_slots, devices, DI),
        ("grp", "fsdp"),
        split_axis=1,
        concat_axis=1,
        tiled=True,
    ).astype(jnp.float32)
    terms = arrived.reshape(devices * cap_slots, DI)
    slot_hot = (
        incoming.T.reshape(-1)[:, None] == jnp.arange(count, dtype=jnp.int32)[None, :]
    ).astype(jnp.float32)
    item_grad = jnp.dot(slot_hot.T, terms, precision=lax.Precision.HIGHEST)
    return (item_embed, user_attention_output[None], item_grad)


def solution(mesh):
    placed = (
        P(("grp", "fsdp"), None, None),
        P("fsdp", None),
        P("fsdp", None),
        P("fsdp", None),
        P(),
        P("fsdp", None),
        P(),
        P("fsdp", None),
        P(("grp", "fsdp"), None, None),
        P(("grp", "fsdp"), None),
        P(("grp", "fsdp"), None, None),
    )
    return jax.shard_map(
        per_device,
        mesh=mesh,
        in_specs=placed,
        out_specs=(
            P(("grp", "fsdp"), None),
            P(("grp", "fsdp"), None, None),
            P(("grp", "fsdp"), None),
        ),
        check_vma=False,
    )
```

```python
import jax
import jax.numpy as jnp
from jax import lax
from jax.experimental import pallas as pl
from jax.experimental.pallas import tpu as pltpu
from jax.sharding import PartitionSpec as P

DI = 2048
IHEADS = 32
IHD = 64
IKV = 4
UHEADS = 32
UHD = 128
ILEN = 256


def stored(values):
    return lax.optimization_barrier(values.astype(jnp.bfloat16))


def rms_scale(values, gain):
    mean_sq = jnp.mean(values * values, axis=-1, keepdims=True)
    return values * lax.rsqrt(mean_sq + 1e-05) * gain


def item_pool(states, key_rows, value_rows, query_rows, item_gain):
    count = states.shape[0]
    group = IHEADS // IKV
    query_heads = query_rows.reshape(count, IKV, group, IHD).astype(jnp.float32)
    key_heads = key_rows.reshape(count, ILEN, IKV, IHD).astype(jnp.float32)
    value_heads = value_rows.reshape(count, ILEN, IKV, IHD).astype(jnp.float32)
    scores = jnp.einsum("igrd,itgd->igrt", query_heads, key_heads) * IHD ** (-0.5)
    weights = stored(jax.nn.softmax(scores, axis=-1)).astype(jnp.float32)
    mixed = jnp.einsum("igrt,itgd->igrd", weights, value_heads).reshape(count, IHEADS * IHD)
    last_row = states[:, ILEN - 1, :].astype(jnp.float32)
    return rms_scale(last_row + mixed, item_gain).astype(jnp.bfloat16)


def user_layer(hidden, user_gain, user_query):
    length_total = hidden.shape[0]
    normed = stored(rms_scale(hidden.astype(jnp.float32), user_gain)).astype(jnp.float32)
    heads = normed.reshape(length_total, UHEADS, UHD)
    query_map = user_query.reshape(UHEADS, UHD, UHD).astype(jnp.float32)
    queries = stored(jnp.einsum("thd,hde->the", heads, query_map)).astype(jnp.float32)
    scores = jnp.einsum("the,she->hts", queries, heads) * UHD ** (-0.5)
    target = jnp.arange(length_total, dtype=jnp.int32)
    causal = target[None, :, None] >= target[None, None, :]
    scores = jnp.where(causal, scores, -1e30)
    weights = stored(jax.nn.softmax(scores, axis=-1)).astype(jnp.float32)
    mixed = jnp.einsum("hts,shd->thd", weights, heads).reshape(length_total, UHEADS * UHD)
    return (hidden.astype(jnp.float32) + mixed).astype(jnp.bfloat16)


def _pack_halves(*refs):
    sources, out = refs[:-1], refs[-1]
    first = lax.axis_index("grp") == 0
    column = 0
    for i, src in enumerate(sources):
        if i == len(sources) - 1:
            rows = src.shape[0] // 2
            width = src.shape[1]
            low, high = src[:rows, :], src[rows:, :]
        else:
            width = src.shape[1] // 2
            low, high = src[:, :width], src[:, width:]
        out[:, column : column + width] = jnp.where(first, low, high)
        column += width


def pack_halves(sources):
    total = sum(w.shape[1] // 2 for w in sources[:-1]) + sources[-1].shape[1]
    return pl.pallas_call(
        _pack_halves,
        out_shape=jax.ShapeDtypeStruct((sources[0].shape[0], total), sources[0].dtype),
    )(*sources)


def serve_rows(requests, lookup_matrix):
    chosen_items = (
        requests[..., None] == jnp.arange(lookup_matrix.shape[0], dtype=jnp.int32)
    ).astype(lookup_matrix.dtype)
    return jnp.einsum(
        "ltj,jy->lty", chosen_items, lookup_matrix, preferred_element_type=jnp.float32
    ).astype(lookup_matrix.dtype)


def per_device(
    item_states,
    w_query,
    w_key,
    w_value,
    item_gain,
    w_adapt,
    user_gain,
    user_query,
    hist_owner,
    history_position_index,
    cotangent,
):
    groups = lax.axis_size("grp")
    shards = lax.axis_size("fsdp")
    devices = groups * shards
    count = item_states.shape[0]
    flat = item_states.reshape(count * ILEN, DI)
    last_row = item_states[:, ILEN - 1, :]
    side = lax.axis_index("grp")

    sources = [w_key, w_value, w_query, w_adapt, user_query]
    widths = [w.shape[1] // 2 for w in sources[:-1]] + [user_query.shape[1]]
    ends = [sum(widths[: i + 1]) for i in range(len(widths))]
    gathered = lax.all_gather(
        pack_halves(sources), ("grp", "fsdp"), axis=0, tiled=True
    ).reshape(groups, DI, ends[-1])
    kv_sum = jnp.einsum(
        "td,gdc->tgc", flat, gathered[:, :, : ends[1]], preferred_element_type=jnp.float32
    )
    key_sum = kv_sum[:, :, : widths[0]].reshape(flat.shape[0], -1)
    summed_value = kv_sum[:, :, widths[0] :].reshape(flat.shape[0], -1)
    query_sum = jnp.einsum(
        "id,gdc->igc", last_row, gathered[:, :, ends[1] : ends[2]], preferred_element_type=jnp.float32
    ).reshape(count, -1)
    adapter_halves = gathered[:, :, ends[2] : ends[3]]
    query_map = (
        gathered[:, :, ends[3] :]
        .reshape(groups, shards, -1, user_query.shape[1])
        .transpose(1, 0, 2, 3)
        .reshape(-1, user_query.shape[1])
    )
    item_embed = item_pool(
        item_states, stored(key_sum), stored(summed_value), stored(query_sum), item_gain
    )
    length_total = history_position_index.shape[1]
    cap_slots = max(2, 2 * length_total // devices)
    owner_users = hist_owner[0, :, 0]
    owner_hot = (owner_users[:, None] == jnp.arange(devices, dtype=jnp.int32)[None, :]).astype(
        jnp.int32
    )
    earlier = jnp.cumsum(owner_hot, axis=0) - owner_hot
    rank_in = jnp.sum(owner_hot * earlier, axis=1)
    position = owner_users * cap_slots + rank_in
    request = (
        jnp.full((devices * cap_slots,), count, jnp.int32)
        .at[position]
        .set(history_position_index[0])
    )
    request = request.reshape(devices, cap_slots)
    width = item_embed.shape[1]
    incoming = lax.all_to_all(request, ("grp", "fsdp"), split_axis=0, concat_axis=0, tiled=True)
    found = jnp.take(
        jnp.concatenate([item_embed, jnp.zeros((1, item_embed.shape[1]), item_embed.dtype)], axis=0),
        jnp.clip(incoming, 0, count),
        axis=0,
        mode="clip",
    )
    returned = lax.all_to_all(found, ("grp", "fsdp"), split_axis=0, concat_axis=0, tiled=True)
    fetched = jnp.take(returned.reshape(devices * cap_slots, width), position, axis=0)
    hidden = stored(
        jnp.einsum("td,gdc->tgc", fetched, adapter_halves, preferred_element_type=jnp.float32).reshape(
            fetched.shape[0], -1
        )
    )
    user_attention_output, pull = jax.vjp(
        lambda values: user_layer(values, user_gain, query_map), hidden
    )
    (grad_hidden,) = pull(cotangent[0])
    grad_rows = jnp.einsum(
        "tgc,gdc->td",
        grad_hidden.reshape(grad_hidden.shape[0], groups, -1),
        adapter_halves,
        preferred_element_type=jnp.float32,
    ).astype(jnp.bfloat16)
    slot_of = (
        position[None, :] == jnp.arange(devices * cap_slots, dtype=jnp.int32)[:, None]
    ).astype(grad_rows.dtype)
    outgoing = jnp.dot(slot_of, grad_rows, preferred_element_type=jnp.float32).astype(
        grad_rows.dtype
    )
    arrived = lax.all_to_all(
        outgoing.reshape(devices, cap_slots, DI),
        ("grp", "fsdp"),
        split_axis=0,
        concat_axis=0,
        tiled=True,
    ).astype(jnp.float32)
    terms = arrived.reshape(devices * cap_slots, DI)
    slot_hot = (
        incoming.reshape(-1)[:, None] == jnp.arange(count, dtype=jnp.int32)[None, :]
    ).astype(jnp.float32)
    item_grad = jnp.dot(slot_hot.T, terms, precision=lax.Precision.HIGHEST)
    return (item_embed, user_attention_output[None], item_grad)


def solution(mesh):
    placed = (
        P(("grp", "fsdp"), None, None),
        P("fsdp", None),
        P("fsdp", None),
        P("fsdp", None),
        P(),
        P("fsdp", None),
        P(),
        P("fsdp", None),
        P(("grp", "fsdp"), None, None),
        P(("grp", "fsdp"), None),
        P(("grp", "fsdp"), None, None),
    )
    return jax.shard_map(
        per_device,
        mesh=mesh,
        in_specs=placed,
        out_specs=(
            P(("grp", "fsdp"), None),
            P(("grp", "fsdp"), None, None),
            P(("grp", "fsdp"), None),
        ),
        check_vma=False,
    )
```

```python
import jax
import jax.numpy as jnp
from jax import lax
from jax.experimental import pallas as pl
from jax.experimental.pallas import tpu as pltpu
from jax.sharding import PartitionSpec as P

DI = 2048
IHEADS = 32
IHD = 64
IKV = 4
UHEADS = 32
UHD = 128
ILEN = 256


def stored(values):
    return lax.optimization_barrier(values.astype(jnp.bfloat16))


def rms_scale(values, gain):
    mean_sq = jnp.mean(values * values, axis=-1, keepdims=True)
    return values * lax.rsqrt(mean_sq + 1e-05) * gain


def item_pool(states, key_rows, value_rows, query_rows, item_gain):
    count = states.shape[0]
    group = IHEADS // IKV
    query_heads = query_rows.reshape(count, IKV, group, IHD).astype(jnp.float32)
    key_heads = key_rows.reshape(count, ILEN, IKV, IHD).astype(jnp.float32)
    value_heads = value_rows.reshape(count, ILEN, IKV, IHD).astype(jnp.float32)
    scores = jnp.einsum("igrd,itgd->igrt", query_heads, key_heads) * IHD ** (-0.5)
    weights = stored(jax.nn.softmax(scores, axis=-1)).astype(jnp.float32)
    mixed = jnp.einsum("igrt,itgd->igrd", weights, value_heads).reshape(count, IHEADS * IHD)
    last_row = states[:, ILEN - 1, :].astype(jnp.float32)
    return rms_scale(last_row + mixed, item_gain).astype(jnp.bfloat16)


def user_layer(hidden, user_gain, user_query):
    length_total = hidden.shape[0]
    normed = stored(rms_scale(hidden.astype(jnp.float32), user_gain)).astype(jnp.float32)
    heads = normed.reshape(length_total, UHEADS, UHD)
    query_map = user_query.reshape(UHEADS, UHD, UHD).astype(jnp.float32)
    queries = stored(jnp.einsum("thd,hde->the", heads, query_map)).astype(jnp.float32)
    scores = jnp.einsum("the,she->hts", queries, heads) * UHD ** (-0.5)
    target = jnp.arange(length_total, dtype=jnp.int32)
    causal = target[None, :, None] >= target[None, None, :]
    scores = jnp.where(causal, scores, -1e30)
    weights = stored(jax.nn.softmax(scores, axis=-1)).astype(jnp.float32)
    mixed = jnp.einsum("hts,shd->thd", weights, heads).reshape(length_total, UHEADS * UHD)
    return (hidden.astype(jnp.float32) + mixed).astype(jnp.bfloat16)


def _pack_halves(*refs):
    sources, out = refs[:-1], refs[-1]
    first = lax.axis_index("grp") == 0
    column = 0
    for i, src in enumerate(sources):
        if i == len(sources) - 1:
            rows = src.shape[0] // 2
            width = src.shape[1]
            low, high = src[:rows, :], src[rows:, :]
        else:
            width = src.shape[1] // 2
            low, high = src[:, :width], src[:, width:]
        out[:, column : column + width] = jnp.where(first, low, high)
        column += width


def pack_halves(sources):
    total = sum(w.shape[1] // 2 for w in sources[:-1]) + sources[-1].shape[1]
    return pl.pallas_call(
        _pack_halves,
        out_shape=jax.ShapeDtypeStruct((sources[0].shape[0], total), sources[0].dtype),
    )(*sources)


def serve_rows(requests, lookup_matrix):
    chosen_items = (
        requests[..., None] == jnp.arange(lookup_matrix.shape[0], dtype=jnp.int32)
    ).astype(lookup_matrix.dtype)
    return jnp.einsum(
        "ltj,jy->lty", chosen_items, lookup_matrix, preferred_element_type=jnp.float32
    ).astype(lookup_matrix.dtype)


def per_device(
    item_states,
    w_query,
    w_key,
    w_value,
    item_gain,
    w_adapt,
    user_gain,
    user_query,
    hist_owner,
    history_position_index,
    cotangent,
):
    groups = lax.axis_size("grp")
    shards = lax.axis_size("fsdp")
    devices = groups * shards
    count = item_states.shape[0]
    flat = item_states.reshape(count * ILEN, DI)
    last_row = item_states[:, ILEN - 1, :]
    side = lax.axis_index("grp")

    sources = [w_key, w_value, w_query, w_adapt, user_query]
    widths = [w.shape[1] // 2 for w in sources[:-1]] + [user_query.shape[1]]
    ends = [sum(widths[: i + 1]) for i in range(len(widths))]
    gathered = lax.all_gather(
        pack_halves(sources), ("grp", "fsdp"), axis=0, tiled=True
    ).reshape(groups, DI, ends[-1])
    kv_sum = jnp.einsum(
        "td,gdc->tgc", flat, gathered[:, :, : ends[1]], preferred_element_type=jnp.float32
    )
    key_sum = kv_sum[:, :, : widths[0]].reshape(flat.shape[0], -1)
    summed_value = kv_sum[:, :, widths[0] :].reshape(flat.shape[0], -1)
    query_sum = jnp.einsum(
        "id,gdc->igc", last_row, gathered[:, :, ends[1] : ends[2]], preferred_element_type=jnp.float32
    ).reshape(count, -1)
    adapter_halves = gathered[:, :, ends[2] : ends[3]]
    query_map = (
        gathered[:, :, ends[3] :]
        .reshape(groups, shards, -1, user_query.shape[1])
        .transpose(1, 0, 2, 3)
        .reshape(-1, user_query.shape[1])
    )
    item_embed = item_pool(
        item_states, stored(key_sum), stored(summed_value), stored(query_sum), item_gain
    )
    length_total = history_position_index.shape[1]
    cap_slots = max(2, 2 * length_total // devices)
    owner_users = hist_owner[0, :, 0]
    owner_hot = (owner_users[:, None] == jnp.arange(devices, dtype=jnp.int32)[None, :]).astype(
        jnp.int32
    )
    earlier = jnp.cumsum(owner_hot, axis=0) - owner_hot
    rank_in = jnp.sum(owner_hot * earlier, axis=1)
    position = owner_users * cap_slots + rank_in
    request = (
        jnp.full((devices * cap_slots,), count, jnp.int32)
        .at[position]
        .set(history_position_index[0])
    )
    request = request.reshape(devices, cap_slots)
    width = item_embed.shape[1]
    incoming = lax.all_to_all(request, ("grp", "fsdp"), split_axis=0, concat_axis=0, tiled=True)
    found = serve_rows(incoming, item_embed)
    returned = lax.all_to_all(found, ("grp", "fsdp"), split_axis=0, concat_axis=0, tiled=True)
    fetched = jnp.take(returned.reshape(devices * cap_slots, width), position, axis=0)
    hidden = stored(
        jnp.concatenate(
            [jnp.dot(fetched, adapter_halves[g], preferred_element_type=jnp.float32) for g in range(groups)],
            axis=1,
        )
    )
    user_attention_output, pull = jax.vjp(
        lambda values: user_layer(values, user_gain, query_map), hidden
    )
    (grad_hidden,) = pull(cotangent[0])
    grad_rows = jnp.einsum(
        "tgc,gdc->td",
        grad_hidden.reshape(grad_hidden.shape[0], groups, -1),
        adapter_halves,
        preferred_element_type=jnp.float32,
    ).astype(jnp.bfloat16)
    slot_of = (
        position[None, :] == jnp.arange(devices * cap_slots, dtype=jnp.int32)[:, None]
    ).astype(grad_rows.dtype)
    outgoing = jnp.dot(slot_of, grad_rows, preferred_element_type=jnp.float32).astype(
        grad_rows.dtype
    )
    arrived = lax.all_to_all(
        outgoing.reshape(devices, cap_slots, DI),
        ("grp", "fsdp"),
        split_axis=0,
        concat_axis=0,
        tiled=True,
    ).astype(jnp.float32)
    terms = arrived.reshape(devices * cap_slots, DI)
    slot_hot = (
        incoming.reshape(-1)[:, None] == jnp.arange(count, dtype=jnp.int32)[None, :]
    ).astype(jnp.float32)
    item_grad = jnp.dot(slot_hot.T, terms, precision=lax.Precision.HIGHEST)
    return (item_embed, user_attention_output[None], item_grad)


def solution(mesh):
    placed = (
        P(("grp", "fsdp"), None, None),
        P("fsdp", None),
        P("fsdp", None),
        P("fsdp", None),
        P(),
        P("fsdp", None),
        P(),
        P("fsdp", None),
        P(("grp", "fsdp"), None, None),
        P(("grp", "fsdp"), None),
        P(("grp", "fsdp"), None, None),
    )
    return jax.shard_map(
        per_device,
        mesh=mesh,
        in_specs=placed,
        out_specs=(
            P(("grp", "fsdp"), None),
            P(("grp", "fsdp"), None, None),
            P(("grp", "fsdp"), None),
        ),
        check_vma=False,
    )
```
